256 devices in a mesh: patch: 32 (over x, y, z_hi), stream: 8 (over z_lo, core).
Axes of the slice: x: 4, y: 4, z: 8 (z_hi: 2, z_lo: 4; z = z_hi * 4 + z_lo), core: 2. Of those that a mesh axis runs over, the one named last changes fastest.
Arguments:
- exposures: bfloat16 [4, 8, 512, 8, 4096], P(None, 'stream', 'patch'), may hold values from -6 to 6
- owners: int32 [4, 8, 512, 2], P(None, 'stream', 'patch'), may hold values from 0 to 31, all different within a row; in each aligned block of 16 rows (0 to 15, 16 to 31, ..., all dimensions but the last counted through in order) at most 2 rows name the same one
- offsets: int32 [4, 8, 512, 2], P(None, 'stream', 'patch'), may hold values from 0 to 56
- visit_shift: float32 [4, 8, 2], P(None, 'stream'), may hold values from 0.05 to 0.95
- visit_weight: float32 [4, 8], P(None, 'stream'), may hold values from 0.25 to 4
- psf_class: int32 [4, 8], P(None, 'stream'), may hold values from 0 to 7
- coef_table: float32 [8, 16], replicated, may hold values from -0.18 to 0.18
- basis_x: float32 [16, 31], replicated, may hold values from -1 to 1
- basis_y: float32 [16, 31], replicated, may hold values from -1 to 1
Outputs:
- coadd: float32 [2048, 4096], P(('patch', 'stream'))
The draws below stay inside these ranges and needn't reach their ends.
Inputs may be any that keep to these rules, and one draw needn't show every extreme that they name: `owners`: each row names 2 different patches; in each step the 16 strips of one holder name one patch at most 2 times, a bound that some block reaches.
All inputs are finite; a program needn't handle non-finite values.
Results may differ from the reference program's by a relative error of at most 0.0062.
Values may be sent and summed in bfloat16 or wider, within the bound.
No kernel may reach another device: no remote copies, remote signals or barrier semaphores. Data moves between devices by JAX's collectives and lax.ppermute only.
A program may use at most 128 MiB of HBM per device.

```python
import math
import jax
import jax.numpy as jnp
import numpy as np
from jax import lax

COLS = 4096
BASES = 16
TAPS = 31
STRIP_ROWS = 8
FANOUT = 2
CAP = 2
STRIPS = 16
STEPS = 4
CLASSES = 8
SLAB_ROWS = 64
HOLD = 512
N_PATCH = 32
N_STREAM = 8


def plant(result, stream_key, low, high):
    spot = [jax.random.randint(jax.random.fold_in(stream_key, axis), (), 0, length) for axis, length in enumerate(result.shape)]
    longest = result.shape.index(max(result.shape))
    beside = spot[:longest] + [(spot[longest] + 1) % result.shape[longest]] + spot[longest + 1:]
    return result.at[tuple(spot)].set(low).at[tuple(beside)].set(high)


def levels(key, shape, shards, low, largest):
    level, own = 1.0, jax.random.fold_in(key, 6)
    for position, shards_of in shards:
        steps = jnp.exp(jax.random.uniform(jax.random.fold_in(own, position), (shards_of,), jnp.float32, low / len(shards), largest / len(shards)))
        level = level * jnp.repeat(steps, shape[position] // shards_of).reshape([-1 if axis == position else 1 for axis in range(len(shape))])
    return level


def shared_out(stream_key, own, number, rows, number_of, top, limit, lean):
    order = jax.random.permutation(stream_key, number_of)
    packed, ordinary = shares(number_of, rows * top, limit, lean, True), shares(number_of, rows * top, limit, lean, False)
    places = jnp.arange(number_of)

    def named(tallies, turn):
        used = int((tallies > 0).sum())
        fixed = max(1, used // 4)
        moved = fixed + (places - fixed + turn * (used - fixed)) % max(1, number_of - fixed)
        return jnp.zeros((number_of,), jnp.int32).at[order[jnp.where(places < fixed, places, moved)]].set(jnp.asarray(tallies, jnp.int32))

    tallies = jnp.where(number % 4 == 0, named(packed, number // 4), named(ordinary, number - number // 4 - 1))
    mixed = jax.random.permutation(jax.random.fold_in(own, 3), number_of)
    donor, receiver = mixed[0:number_of // 2 * 2:2], mixed[1:number_of // 2 * 2:2]
    margin = jnp.minimum(tallies[donor] - 1, limit - tallies[receiver]) // 2
    margin = jnp.where((donor == order[0]) | (receiver == order[0]) | (tallies[receiver] == 0), 0, jnp.maximum(margin, 0))
    moved = jax.random.randint(jax.random.fold_in(own, 4), (number_of // 2,), 0, 1 << 20) % (margin + 1)
    tallies = tallies.at[donor].add(-moved).at[receiver].add(moved)
    members = jnp.searchsorted(jnp.cumsum(tallies), jnp.arange(rows * top), side="right").astype(jnp.int32)
    table = members.reshape(top, rows).T
    table = table[jax.random.permutation(jax.random.fold_in(own, 1), rows)]
    turn = jax.random.randint(jax.random.fold_in(own, 2), (rows, 1), 0, top)
    return jnp.take_along_axis(table, (jnp.arange(top)[None, :] + turn) % top, axis=1)


def shares(amount, total, most, skew, full):
    loads = [(1 << 20) // math.isqrt(standing ** skew) + 1 for standing in range(1, amount + 1)]
    largest = most if full else min(most, max(-(-total // amount), total * loads[0] // sum(loads)))
    least = 1 if total - largest >= amount - 1 else 0
    holding, spare = [largest] + [least] * (amount - 1), total - largest - least * (amount - 1)
    while spare > 0:
        free = [i for i in range(1, amount) if holding[i] < largest] or [i for i in range(1, amount) if holding[i] < most]
        pool, budget = sum([loads[i] for i in free]), spare
        for i in free:
            extra = min(most - holding[i], max(1, budget * loads[i] // pool), spare)
            holding[i] = holding[i] + extra
            spare = spare - extra
    return np.array(holding)


def bell_draw(stream_key, extent, spread, reach, cuts=(), kind=jnp.bfloat16):
    result = jax.random.normal(stream_key, extent, jnp.float32) * spread
    if len(cuts) > 0:
        result = levels(stream_key, extent, cuts, -0.22, 0.18) * result
    return jnp.clip(result, min=-reach, max=reach).astype(kind)


def setup_inputs(seed: int = 0) -> dict:
    keys = jax.random.split(jax.random.key(seed), 10)
    exposures = bell_draw(keys[0], (STEPS, N_STREAM, HOLD, STRIP_ROWS, COLS), 1.0, 6.0, ((1, 8), (2, 32)))
    owners_keys = jax.random.split(jax.random.fold_in(keys[1], 1), STEPS * N_STREAM * HOLD // STRIPS)
    owners_turns = jax.random.permutation(jax.random.fold_in(keys[1], 3), STEPS * N_STREAM * HOLD // STRIPS)
    owners = jax.vmap(lambda own, number: shared_out(jax.random.fold_in(keys[1], 2), own, number, STRIPS, N_PATCH, FANOUT, CAP, 2))(owners_keys, owners_turns).reshape((STEPS, N_STREAM, HOLD, FANOUT))
    offsets = plant(jax.random.randint(keys[2], (STEPS, N_STREAM, HOLD, FANOUT), 0, SLAB_ROWS - STRIP_ROWS + 1), jax.random.fold_in(keys[2], 1), 0, SLAB_ROWS - STRIP_ROWS).astype(jnp.int32)
    visit_shift = jnp.clip(0.05 + 0.9 * jax.random.uniform(keys[3], (STEPS, N_STREAM, 2), jnp.float32) ** levels(keys[3], (STEPS, N_STREAM, 2), ((1, 8),), -0.2, 0.2), 0.05, 0.95)
    visit_weight = jnp.clip(jnp.exp(math.log(4.0) - 2.7725887 * jax.random.uniform(keys[4], (STEPS, N_STREAM), jnp.float32) ** levels(keys[4], (STEPS, N_STREAM), ((1, 8),), -0.2, 0.2)), 0.25, 4.0)
    psf_class = plant(jax.random.randint(keys[5], (STEPS, N_STREAM), 0, CLASSES), jax.random.fold_in(keys[5], 1), 0, CLASSES - 1).astype(jnp.int32)
    coef_table = bell_draw(keys[6], (CLASSES, BASES), 0.03, 0.18, (), jnp.float32)
    basis_x = bell_draw(keys[7], (BASES, TAPS), TAPS ** -0.5, 1.0, (), jnp.float32)
    basis_y = bell_draw(keys[8], (BASES, TAPS), TAPS ** -0.5, 1.0, (), jnp.float32)
    return {"exposures": exposures, "owners": owners, "offsets": offsets, "visit_shift": visit_shift, "visit_weight": visit_weight, "psf_class": psf_class, "coef_table": coef_table, "basis_x": basis_x, "basis_y": basis_y}


def lanczos_taps(fraction):
    distance = jnp.arange(6, dtype=jnp.int32).astype(jnp.float32) - 2.0 - fraction
    values = jnp.sinc(distance) * jnp.sinc(distance / 3.0)
    return values / jnp.sum(values)


def combined_taps(basis_rows, warp_x):
    summed = jnp.zeros((basis_rows.shape[0], basis_rows.shape[1] + 5), jnp.float32)
    for tap_slot in range(6):
        summed = summed + jnp.pad(basis_rows * warp_x[tap_slot], ((0, 0), (tap_slot, 5 - tap_slot)))
    return summed


def row_filter(slab_image, tap_values):
    row_count = slab_image.shape[0]
    width = slab_image.shape[1]
    blocks = width // 128
    padded = jnp.pad(slab_image, ((0, 0), (32, 96)))
    front_part = padded[:, :width].reshape(row_count, blocks, 128)
    second = padded[:, 128:width + 128].reshape(row_count, blocks, 128)[:, :, :64]
    windows = jnp.concatenate([front_part, second], axis=2)
    band_index = jnp.arange(192, dtype=jnp.int32)[:, None] - jnp.arange(128, dtype=jnp.int32)[None, :] - 15
    selector = (band_index[:, :, None] == jnp.arange(tap_values.shape[1], dtype=jnp.int32)[None, None, :]).astype(jnp.float32)
    band_matrix = jnp.einsum("aom,bm->bao", selector, tap_values.astype(jnp.float32), precision=lax.Precision.HIGHEST)
    band_matrix = band_matrix.astype(jnp.bfloat16)
    filtered = jnp.einsum("rna,bao->brno", windows.astype(jnp.float32), band_matrix.astype(jnp.float32), precision=lax.Precision.HIGHEST)
    return filtered.astype(jnp.bfloat16).reshape(tap_values.shape[0] * row_count, width)


def mixing(weight, coeffs, basis_y, row_count):
    tap_index = jnp.arange(row_count, dtype=jnp.int32)[None, :] - jnp.arange(row_count, dtype=jnp.int32)[:, None] + 15
    selector = (tap_index[:, :, None] == jnp.arange(basis_y.shape[1], dtype=jnp.int32)[None, None, :]).astype(jnp.float32)
    kernel_table = jnp.einsum("rsj,bj->rbs", selector, basis_y, precision=lax.Precision.HIGHEST)
    kernel_table = kernel_table * (weight * coeffs)[None, :, None]
    return kernel_table.astype(jnp.bfloat16).reshape(row_count, -1)


def reference(exposures, owners, offsets, visit_shift, visit_weight, psf_class, coef_table, basis_x, basis_y):
    row_ids = jnp.arange(STRIP_ROWS, dtype=jnp.int32)
    visit_items = (exposures.reshape(STEPS * N_STREAM, HOLD, STRIP_ROWS, COLS),
                   owners.reshape(STEPS * N_STREAM, HOLD, FANOUT),
                   offsets.reshape(STEPS * N_STREAM, HOLD, FANOUT),
                   visit_shift.reshape(STEPS * N_STREAM, 2),
                   visit_weight.reshape(STEPS * N_STREAM),
                   psf_class.reshape(STEPS * N_STREAM))

    def visit(coadd_sum, items):
        strips, owner_table, offset_table, shifts, weight, psf_index = items
        warp_x = lanczos_taps(shifts[0])
        warp_y = lanczos_taps(shifts[1])
        tap_index = row_ids[None, :] - row_ids[:, None] + 2
        ymat = jnp.sum((tap_index[:, :, None] == jnp.arange(6, dtype=jnp.int32)[None, None, :]).astype(jnp.float32) * warp_y, axis=2)
        ymat = ymat.astype(jnp.bfloat16)
        warped = jnp.einsum("ij,hjc->hic", ymat.astype(jnp.float32), strips.astype(jnp.float32), precision=lax.Precision.HIGHEST)
        slab_stack = jnp.zeros((N_PATCH * SLAB_ROWS, COLS), jnp.float32)
        for owner_slot in range(FANOUT):
            targets = (owner_table[:, owner_slot] * SLAB_ROWS + offset_table[:, owner_slot])[:, None] + row_ids[None, :]
            slab_stack = slab_stack.at[targets.reshape(-1)].add(warped.reshape(-1, COLS))
        slab_stack = slab_stack.astype(jnp.bfloat16).reshape(N_PATCH, SLAB_ROWS, COLS)
        tap_values = combined_taps(basis_x, warp_x).astype(jnp.bfloat16)
        class_hits = (psf_index == jnp.arange(CLASSES, dtype=jnp.int32)).astype(jnp.float32)
        coeffs = jnp.sum(class_hits[:, None] * coef_table, axis=0)
        mix_matrix = mixing(weight, coeffs, basis_y, SLAB_ROWS)

        def patch_term(slab_image):
            filtered = row_filter(slab_image, tap_values)
            return jnp.dot(mix_matrix.astype(jnp.float32), filtered.astype(jnp.float32), precision=lax.Precision.HIGHEST)

        terms = lax.map(patch_term, slab_stack)
        return coadd_sum + terms.reshape(N_PATCH * SLAB_ROWS, COLS), None

    coadd_sum, _ = lax.scan(visit, jnp.zeros((N_PATCH * SLAB_ROWS, COLS), jnp.float32), visit_items)
    return coadd_sum
```

```python
import jax
import jax.numpy as jnp
from jax import lax
from jax.sharding import PartitionSpec as P

CAP = 2
SLAB_ROWS = 64


def lanczos_taps(fraction):
    distance = jnp.arange(6, dtype=jnp.int32).astype(jnp.float32) - 2.0 - fraction
    values = jnp.sinc(distance) * jnp.sinc(distance / 3.0)
    return values / jnp.sum(values)


def combined_taps(basis_rows, warp_x):
    summed = jnp.zeros((basis_rows.shape[0], basis_rows.shape[1] + 5), jnp.float32)
    for tap_slot in range(6):
        summed = summed + jnp.pad(basis_rows * warp_x[tap_slot], ((0, 0), (tap_slot, 5 - tap_slot)))
    return summed


def toeplitz(period, count):
    length = period.shape[-1] - 1
    tiled = jnp.tile(period, [1] * (period.ndim - 1) + [count])
    return tiled[..., : count * length].reshape(period.shape[:-1] + (count, length))


def row_filter(slab_image, tap_values):
    row_count = slab_image.shape[0]
    width = slab_image.shape[1]
    blocks = width // 128
    padded = jnp.pad(slab_image, ((0, 0), (32, 96)))
    front_part = padded[:, :width].reshape(row_count, blocks, 128)
    second = padded[:, 128 : width + 128].reshape(row_count, blocks, 128)[:, :, :64]
    windows = jnp.concatenate([front_part, second], axis=2)
    taps = tap_values.shape[1]
    band_rows = jnp.pad(tap_values, ((0, 0), (15, 193 - 15 - taps)))
    band_matrix = toeplitz(band_rows, 128)
    filtered = jnp.einsum("rna,boa->brno", windows, band_matrix, preferred_element_type=jnp.float32)
    return filtered.astype(jnp.bfloat16).reshape(tap_values.shape[0] * row_count, width)


def mixing(weight, coeffs, basis_y, row_count):
    reach = basis_y.shape[1] // 2
    period = jnp.pad(basis_y, ((0, 0), (0, row_count + reach + 1 - basis_y.shape[1])))
    kernel_table = toeplitz(period, row_count)[:, :, reach:]
    kernel_table = kernel_table * (weight * coeffs)[:, None, None]
    return kernel_table.astype(jnp.bfloat16).transpose(1, 0, 2).reshape(row_count, -1)


def pack(strips, owner_table, offset_table, patches):
    strip_count = strips.shape[0]
    fanout = owner_table.shape[1]
    target = owner_table.reshape(-1)
    target_hits = (target[:, None] == jnp.arange(patches, dtype=jnp.int32)[None, :]).astype(
        jnp.int32
    )
    earlier = jnp.cumsum(target_hits, axis=0) - target_hits
    position = jnp.sum(earlier * target_hits, axis=1)
    slot_index = target * CAP + position
    matches = (slot_index[None, :] == jnp.arange(patches * CAP, dtype=jnp.int32)[:, None]).astype(
        jnp.int32
    )
    strip_select = jnp.sum(matches.reshape(patches * CAP, strip_count, fanout), axis=2).astype(
        jnp.bfloat16
    )
    outgoing = jnp.dot(
        strip_select, strips.reshape(strip_count, -1), preferred_element_type=jnp.bfloat16
    )
    filled = jnp.sum(matches, axis=1)
    slot_offset = jnp.sum(matches * offset_table.reshape(-1)[None, :], axis=1) + (filled - 1) * (
        SLAB_ROWS + 8
    )
    return (
        outgoing.reshape(patches, CAP, strips.shape[1], strips.shape[2]),
        slot_offset.reshape(patches, CAP),
    )


def place(received, recv_off, warp_y):
    strip_rows = received.shape[-2]
    width = received.shape[-1]
    starts = recv_off.reshape(-1)
    local_row = jnp.arange(SLAB_ROWS, dtype=jnp.int32)[:, None] - starts[None, :]
    inside = (local_row >= 0) & (local_row < strip_rows)
    tap_index = jnp.arange(strip_rows, dtype=jnp.int32)[None, None, :] - local_row[:, :, None] + 2
    tap_hits = (tap_index[:, :, :, None] == jnp.arange(6, dtype=jnp.int32)).astype(jnp.float32)
    tap_values = jnp.sum(tap_hits * warp_y, axis=3)
    tap_values = (
        jnp.where(inside[:, :, None], tap_values, 0.0).astype(jnp.bfloat16).reshape(SLAB_ROWS, -1)
    )
    return jnp.dot(tap_values, received.reshape(-1, width), preferred_element_type=jnp.float32)


def visit_term(received, recv_off, shifts, weight, psf_index, coef_table, basis_x, basis_y):
    warp_x = lanczos_taps(shifts[0])
    warp_y = lanczos_taps(shifts[1])
    slab_image = place(received, recv_off, warp_y).astype(jnp.bfloat16)
    tap_values = combined_taps(basis_x, warp_x).astype(jnp.bfloat16)
    filtered = row_filter(slab_image, tap_values)
    class_hits = (psf_index == jnp.arange(coef_table.shape[0], dtype=jnp.int32)).astype(jnp.float32)
    coeffs = jnp.sum(class_hits[:, None] * coef_table, axis=0)
    mix_matrix = mixing(weight, coeffs, basis_y, SLAB_ROWS)
    return jnp.dot(mix_matrix, filtered, preferred_element_type=jnp.float32)


def shards(
    exposures, owners, offsets, visit_shift, visit_weight, psf_class, coef_table, basis_x, basis_y
):
    patches = lax.axis_size("patch")
    streams = lax.axis_size("stream")
    step_count = exposures.shape[0]
    width = exposures.shape[4]
    packed = [
        pack(exposures[step_index, 0], owners[step_index, 0], offsets[step_index, 0], patches)
        for step_index in range(step_count)
    ]
    slot_offsets = jnp.stack([slot_offset for _, slot_offset in packed], axis=1)
    recv_offsets = lax.all_to_all(slot_offsets, "patch", split_axis=0, concat_axis=0, tiled=True)
    partial_sum = jnp.zeros((SLAB_ROWS, width), jnp.float32)
    for step_index in range(step_count):
        received = lax.all_to_all(
            packed[step_index][0], "patch", split_axis=0, concat_axis=0, tiled=True
        )
        visit_part = visit_term(
            received,
            recv_offsets[:, step_index],
            visit_shift[step_index, 0],
            visit_weight[step_index, 0],
            psf_class[step_index, 0],
            coef_table,
            basis_x,
            basis_y,
        )
        partial_sum = partial_sum + visit_part
    share_rows = SLAB_ROWS // streams
    pieces = lax.all_to_all(
        partial_sum.reshape(streams, share_rows, width), "stream", split_axis=0, concat_axis=0,
        tiled=True,
    )
    return jnp.sum(pieces, axis=0)


def solution(mesh):
    placed = (
        P(None, "stream", "patch", None, None),
        P(None, "stream", "patch", None),
        P(None, "stream", "patch", None),
        P(None, "stream", None),
        P(None, "stream"),
        P(None, "stream"),
        P(),
        P(),
        P(),
    )
    return jax.shard_map(
        shards, mesh=mesh, in_specs=placed, out_specs=P(("patch", "stream"), None), check_vma=False
    )
```

```python
import jax
import jax.numpy as jnp
from jax import lax
from jax.sharding import PartitionSpec as P

CAP = 2
SLAB_ROWS = 64


def lanczos_taps(fraction):
    distance = jnp.arange(6, dtype=jnp.int32).astype(jnp.float32) - 2.0 - fraction
    values = jnp.sinc(distance) * jnp.sinc(distance / 3.0)
    return values / jnp.sum(values)


def combined_taps(basis_rows, warp_x):
    summed = jnp.zeros((basis_rows.shape[0], basis_rows.shape[1] + 5), jnp.float32)
    for tap_slot in range(6):
        summed = summed + jnp.pad(basis_rows * warp_x[tap_slot], ((0, 0), (tap_slot, 5 - tap_slot)))
    return summed


def toeplitz(period, count):
    length = period.shape[-1] - 1
    tiled = jnp.tile(period, [1] * (period.ndim - 1) + [count])
    return tiled[..., : count * length].reshape(period.shape[:-1] + (count, length))


def row_filter(slab_image, tap_values):
    row_count = slab_image.shape[0]
    width = slab_image.shape[1]
    blocks = width // 128
    padded = jnp.pad(slab_image, ((0, 0), (32, 96)))
    front_part = padded[:, :width].reshape(row_count, blocks, 128)
    second = padded[:, 128 : width + 128].reshape(row_count, blocks, 128)[:, :, :64]
    windows = jnp.concatenate([front_part, second], axis=2)
    taps = tap_values.shape[1]
    band_rows = jnp.pad(tap_values, ((0, 0), (15, 193 - 15 - taps)))
    band_matrix = toeplitz(band_rows, 128)
    filtered = jnp.einsum("rna,boa->brno", windows, band_matrix, preferred_element_type=jnp.float32)
    return filtered.astype(jnp.bfloat16).reshape(tap_values.shape[0] * row_count, width)


def mixing(weight, coeffs, basis_y, row_count):
    reach = basis_y.shape[1] // 2
    period = jnp.pad(basis_y, ((0, 0), (0, row_count + reach + 1 - basis_y.shape[1])))
    kernel_table = toeplitz(period, row_count)[:, :, reach:]
    kernel_table = kernel_table * (weight * coeffs)[:, None, None]
    return kernel_table.astype(jnp.bfloat16).transpose(1, 0, 2).reshape(row_count, -1)


def pack(strips, owner_table, offset_table, patches):
    strip_count = strips.shape[0]
    fanout = owner_table.shape[1]
    target = owner_table.reshape(-1)
    target_hits = (target[:, None] == jnp.arange(patches, dtype=jnp.int32)[None, :]).astype(
        jnp.int32
    )
    earlier = jnp.cumsum(target_hits, axis=0) - target_hits
    position = jnp.sum(earlier * target_hits, axis=1)
    slot_index = target * CAP + position
    matches = (slot_index[None, :] == jnp.arange(patches * CAP, dtype=jnp.int32)[:, None]).astype(
        jnp.int32
    )
    strip_select = jnp.sum(matches.reshape(patches * CAP, strip_count, fanout), axis=2).astype(
        jnp.bfloat16
    )
    outgoing = jnp.dot(
        strip_select, strips.reshape(strip_count, -1), preferred_element_type=jnp.bfloat16
    )
    filled = jnp.sum(matches, axis=1)
    slot_offset = jnp.sum(matches * offset_table.reshape(-1)[None, :], axis=1) + (filled - 1) * (
        SLAB_ROWS + 8
    )
    return (
        outgoing.reshape(patches, CAP, strips.shape[1], strips.shape[2]),
        slot_offset.reshape(patches, CAP),
    )


def place(received, recv_off, warp_y):
    strip_rows = received.shape[-2]
    width = received.shape[-1]
    starts = recv_off.reshape(-1)
    local_row = jnp.arange(SLAB_ROWS, dtype=jnp.int32)[:, None] - starts[None, :]
    inside = (local_row >= 0) & (local_row < strip_rows)
    tap_index = jnp.arange(strip_rows, dtype=jnp.int32)[None, None, :] - local_row[:, :, None] + 2
    tap_hits = (tap_index[:, :, :, None] == jnp.arange(6, dtype=jnp.int32)).astype(jnp.float32)
    tap_values = jnp.sum(tap_hits * warp_y, axis=3)
    tap_values = (
        jnp.where(inside[:, :, None], tap_values, 0.0).astype(jnp.bfloat16).reshape(SLAB_ROWS, -1)
    )
    return jnp.dot(tap_values, received.reshape(-1, width), preferred_element_type=jnp.float32)


def visit_term(received, recv_off, shifts, weight, psf_index, coef_table, basis_x, basis_y):
    warp_x = lanczos_taps(shifts[0])
    warp_y = lanczos_taps(shifts[1])
    slab_image = place(received, recv_off, warp_y).astype(jnp.bfloat16)
    tap_values = combined_taps(basis_x, warp_x).astype(jnp.bfloat16)
    filtered = row_filter(slab_image, tap_values)
    class_hits = (psf_index == jnp.arange(coef_table.shape[0], dtype=jnp.int32)).astype(jnp.float32)
    coeffs = jnp.sum(class_hits[:, None] * coef_table, axis=0)
    mix_matrix = mixing(weight, coeffs, basis_y, SLAB_ROWS)
    return jnp.dot(mix_matrix, filtered, preferred_element_type=jnp.float32)


def shards(
    exposures, owners, offsets, visit_shift, visit_weight, psf_class, coef_table, basis_x, basis_y
):
    patches = lax.axis_size("patch")
    streams = lax.axis_size("stream")
    step_count = exposures.shape[0]
    width = exposures.shape[4]
    packed = [
        pack(exposures[step_index, 0], owners[step_index, 0], offsets[step_index, 0], patches)
        for step_index in range(step_count)
    ]
    slot_offsets = jnp.stack([slot_offset for _, slot_offset in packed], axis=1)
    recv_offsets = lax.all_to_all(slot_offsets, "patch", split_axis=0, concat_axis=0, tiled=True)
    outgoing = [strips_out for strips_out, _ in packed]
    received = [None] * step_count
    for step_index in range(min(2, step_count)):
        received[step_index] = lax.all_to_all(
            outgoing[step_index], "patch", split_axis=0, concat_axis=0, tiled=True
        )
    partial_sum = jnp.zeros((SLAB_ROWS, width), jnp.float32)
    for step_index in range(step_count):
        visit_part = visit_term(
            received[step_index],
            recv_offsets[:, step_index],
            visit_shift[step_index, 0],
            visit_weight[step_index, 0],
            psf_class[step_index, 0],
            coef_table,
            basis_x,
            basis_y,
        )
        partial_sum = partial_sum + visit_part
        later = step_index + 2
        if later < step_count:
            released, partial_sum = lax.optimization_barrier((outgoing[later], partial_sum))
            received[later] = lax.all_to_all(
                released, "patch", split_axis=0, concat_axis=0, tiled=True
            )
    share_rows = SLAB_ROWS // streams
    pieces = lax.all_to_all(
        partial_sum.reshape(streams, share_rows, width), "stream", split_axis=0, concat_axis=0,
        tiled=True,
    )
    return jnp.sum(pieces, axis=0)


def solution(mesh):
    placed = (
        P(None, "stream", "patch", None, None),
        P(None, "stream", "patch", None),
        P(None, "stream", "patch", None),
        P(None, "stream", None),
        P(None, "stream"),
        P(None, "stream"),
        P(),
        P(),
        P(),
    )
    return jax.shard_map(
        shards, mesh=mesh, in_specs=placed, out_specs=P(("patch", "stream"), None), check_vma=False
    )
```

```python
import jax
import jax.numpy as jnp
from jax import lax
from jax.sharding import PartitionSpec as P
from jax.experimental import pallas as pl

CAP = 2
SLAB_ROWS = 64


def lanczos_taps(fraction):
    distance = jnp.arange(6, dtype=jnp.int32).astype(jnp.float32) - 2.0 - fraction
    values = jnp.sinc(distance) * jnp.sinc(distance / 3.0)
    return values / jnp.sum(values)


def combined_taps(basis_rows, warp_x):
    summed = jnp.zeros((basis_rows.shape[0], basis_rows.shape[1] + 5), jnp.float32)
    for tap_slot in range(6):
        summed = summed + jnp.pad(basis_rows * warp_x[tap_slot], ((0, 0), (tap_slot, 5 - tap_slot)))
    return summed


def toeplitz(period, count):
    length = period.shape[-1] - 1
    tiled = jnp.tile(period, [1] * (period.ndim - 1) + [count])
    return tiled[..., : count * length].reshape(period.shape[:-1] + (count, length))


def row_filter(slab_image, tap_values):
    row_count = slab_image.shape[0]
    width = slab_image.shape[1]
    blocks = width // 128
    padded = jnp.pad(slab_image, ((0, 0), (32, 96)))
    front_part = padded[:, :width].reshape(row_count, blocks, 128)
    second = padded[:, 128 : width + 128].reshape(row_count, blocks, 128)[:, :, :64]
    windows = jnp.concatenate([front_part, second], axis=2)
    taps = tap_values.shape[1]
    band_rows = jnp.pad(tap_values, ((0, 0), (15, 193 - 15 - taps)))
    band_matrix = toeplitz(band_rows, 128)
    filtered = jnp.einsum("rna,boa->brno", windows, band_matrix, preferred_element_type=jnp.float32)
    return filtered.astype(jnp.bfloat16).reshape(tap_values.shape[0] * row_count, width)


def mixing(weight, coeffs, basis_y, row_count):
    reach = basis_y.shape[1] // 2
    period = jnp.pad(basis_y, ((0, 0), (0, row_count + reach + 1 - basis_y.shape[1])))
    kernel_table = toeplitz(period, row_count)[:, :, reach:]
    kernel_table = kernel_table * (weight * coeffs)[:, None, None]
    return kernel_table.astype(jnp.bfloat16).transpose(1, 0, 2).reshape(row_count, -1)


def pack(strips, owner_table, offset_table, patches):
    strip_count = strips.shape[0]
    fanout = owner_table.shape[1]
    target = owner_table.reshape(-1)
    target_hits = (target[:, None] == jnp.arange(patches, dtype=jnp.int32)[None, :]).astype(
        jnp.int32
    )
    earlier = jnp.cumsum(target_hits, axis=0) - target_hits
    position = jnp.sum(earlier * target_hits, axis=1)
    slot_index = target * CAP + position
    matches = (slot_index[None, :] == jnp.arange(patches * CAP, dtype=jnp.int32)[:, None]).astype(
        jnp.int32
    )
    strip_select = jnp.sum(matches.reshape(patches * CAP, strip_count, fanout), axis=2).astype(
        jnp.bfloat16
    )
    outgoing = jnp.dot(
        strip_select, strips.reshape(strip_count, -1), preferred_element_type=jnp.bfloat16
    )
    filled = jnp.sum(matches, axis=1)
    slot_offset = jnp.sum(matches * offset_table.reshape(-1)[None, :], axis=1) + (filled - 1) * (
        SLAB_ROWS + 8
    )
    return (
        outgoing.reshape(patches, CAP, strips.shape[1], strips.shape[2]),
        slot_offset.reshape(patches, CAP),
    )


def place(received, recv_off, warp_y):
    strip_rows = received.shape[-2]
    width = received.shape[-1]
    starts = recv_off.reshape(-1)
    local_row = jnp.arange(SLAB_ROWS, dtype=jnp.int32)[:, None] - starts[None, :]
    inside = (local_row >= 0) & (local_row < strip_rows)
    tap_index = jnp.arange(strip_rows, dtype=jnp.int32)[None, None, :] - local_row[:, :, None] + 2
    tap_hits = (tap_index[:, :, :, None] == jnp.arange(6, dtype=jnp.int32)).astype(jnp.float32)
    tap_values = jnp.sum(tap_hits * warp_y, axis=3)
    tap_values = (
        jnp.where(inside[:, :, None], tap_values, 0.0).astype(jnp.bfloat16).reshape(SLAB_ROWS, -1)
    )
    return jnp.dot(tap_values, received.reshape(-1, width), preferred_element_type=jnp.float32)


LANE = 128
SPAN = 512


def filter_mix_kernel(slab_ref, halo_ref, band_ref, mix_ref, acc_ref, out_ref):
    full = jnp.concatenate([slab_ref[...], halo_ref[...]], axis=1)
    bases = band_ref.shape[1] // LANE
    for block in range(SPAN // LANE):
        window = full[:, block * LANE : block * LANE + 2 * LANE]
        filtered = jnp.dot(window, band_ref[...], preferred_element_type=jnp.float32)
        filtered = filtered.astype(jnp.bfloat16)
        stacked = jnp.concatenate(
            [filtered[:, base * LANE : (base + 1) * LANE] for base in range(bases)], axis=0
        )
        term = jnp.dot(mix_ref[...], stacked, preferred_element_type=jnp.float32)
        out_ref[:, block * LANE : (block + 1) * LANE] = (
            acc_ref[:, block * LANE : (block + 1) * LANE] + term
        )


def filter_mix(slab_image, tap_values, mix_matrix, acc):
    rows, width = slab_image.shape
    bases, taps = tap_values.shape
    padded = jnp.pad(slab_image, ((0, 0), (32, SPAN - 32)))
    band_rows = jnp.pad(tap_values, ((0, 0), (15, 2 * LANE + 1 - 15 - taps)))
    band = toeplitz(band_rows, LANE).transpose(2, 0, 1).reshape(2 * LANE, bases * LANE)
    steps = width // SPAN
    return pl.pallas_call(
        filter_mix_kernel,
        grid=(steps,),
        in_specs=[
            pl.BlockSpec((rows, SPAN), lambda k: (0, k)),
            pl.BlockSpec((rows, LANE), lambda k: (0, (k + 1) * (SPAN // LANE))),
            pl.BlockSpec((2 * LANE, bases * LANE), lambda k: (0, 0)),
            pl.BlockSpec((rows, bases * rows), lambda k: (0, 0)),
            pl.BlockSpec((rows, SPAN), lambda k: (0, k)),
        ],
        out_specs=pl.BlockSpec((rows, SPAN), lambda k: (0, k)),
        out_shape=jax.ShapeDtypeStruct((rows, width), jnp.float32),
        input_output_aliases={4: 0},
    )(padded, padded, band, mix_matrix, acc)


def visit_term(received, recv_off, shifts, weight, psf_index, coef_table, basis_x, basis_y, acc):
    warp_x = lanczos_taps(shifts[0])
    warp_y = lanczos_taps(shifts[1])
    slab_image = place(received, recv_off, warp_y).astype(jnp.bfloat16)
    tap_values = combined_taps(basis_x, warp_x).astype(jnp.bfloat16)
    class_hits = (psf_index == jnp.arange(coef_table.shape[0], dtype=jnp.int32)).astype(jnp.float32)
    coeffs = jnp.sum(class_hits[:, None] * coef_table, axis=0)
    mix_matrix = mixing(weight, coeffs, basis_y, SLAB_ROWS)
    return filter_mix(slab_image, tap_values, mix_matrix, acc)


def shards(
    exposures, owners, offsets, visit_shift, visit_weight, psf_class, coef_table, basis_x, basis_y
):
    patches = lax.axis_size("patch")
    streams = lax.axis_size("stream")
    step_count = exposures.shape[0]
    width = exposures.shape[4]
    packed = [
        pack(exposures[step_index, 0], owners[step_index, 0], offsets[step_index, 0], patches)
        for step_index in range(step_count)
    ]
    slot_offsets = jnp.stack([slot_offset for _, slot_offset in packed], axis=1)
    recv_offsets = lax.all_to_all(slot_offsets, "patch", split_axis=0, concat_axis=0, tiled=True)
    outgoing = [strips_out for strips_out, _ in packed]
    received = [None] * step_count
    for step_index in range(min(2, step_count)):
        received[step_index] = lax.all_to_all(
            outgoing[step_index], "patch", split_axis=0, concat_axis=0, tiled=True
        )
    partial_sum = jnp.zeros((SLAB_ROWS, width), jnp.float32)
    for step_index in range(step_count):
        visit_part = visit_term(
            received[step_index],
            recv_offsets[:, step_index],
            visit_shift[step_index, 0],
            visit_weight[step_index, 0],
            psf_class[step_index, 0],
            coef_table,
            basis_x,
            basis_y,
            partial_sum,
        )
        partial_sum = visit_part
        later = step_index + 2
        if later < step_count:
            released, partial_sum = lax.optimization_barrier((outgoing[later], partial_sum))
            received[later] = lax.all_to_all(
                released, "patch", split_axis=0, concat_axis=0, tiled=True
            )
    share_rows = SLAB_ROWS // streams
    pieces = lax.all_to_all(
        partial_sum.reshape(streams, share_rows, width), "stream", split_axis=0, concat_axis=0,
        tiled=True,
    )
    return jnp.sum(pieces, axis=0)


def solution(mesh):
    placed = (
        P(None, "stream", "patch", None, None),
        P(None, "stream", "patch", None),
        P(None, "stream", "patch", None),
        P(None, "stream", None),
        P(None, "stream"),
        P(None, "stream"),
        P(),
        P(),
        P(),
    )
    return jax.shard_map(
        shards, mesh=mesh, in_specs=placed, out_specs=P(("patch", "stream"), None), check_vma=False
    )
```

```python
import jax
import jax.numpy as jnp
from jax import lax
from jax.sharding import PartitionSpec as P
from jax.experimental import pallas as pl

CAP = 2
SLAB_ROWS = 64


def lanczos_taps(fraction):
    distance = jnp.arange(6, dtype=jnp.int32).astype(jnp.float32) - 2.0 - fraction
    values = jnp.sinc(distance) * jnp.sinc(distance / 3.0)
    return values / jnp.sum(values)


def combined_taps(basis_rows, warp_x):
    summed = jnp.zeros((basis_rows.shape[0], basis_rows.shape[1] + 5), jnp.float32)
    for tap_slot in range(6):
        summed = summed + jnp.pad(basis_rows * warp_x[tap_slot], ((0, 0), (tap_slot, 5 - tap_slot)))
    return summed


def toeplitz(period, count):
    length = period.shape[-1] - 1
    tiled = jnp.tile(period, [1] * (period.ndim - 1) + [count])
    return tiled[..., : count * length].reshape(period.shape[:-1] + (count, length))


def row_filter(slab_image, tap_values):
    row_count = slab_image.shape[0]
    width = slab_image.shape[1]
    blocks = width // 128
    padded = jnp.pad(slab_image, ((0, 0), (32, 96)))
    front_part = padded[:, :width].reshape(row_count, blocks, 128)
    second = padded[:, 128 : width + 128].reshape(row_count, blocks, 128)[:, :, :64]
    windows = jnp.concatenate([front_part, second], axis=2)
    taps = tap_values.shape[1]
    band_rows = jnp.pad(tap_values, ((0, 0), (15, 193 - 15 - taps)))
    band_matrix = toeplitz(band_rows, 128)
    filtered = jnp.einsum("rna,boa->brno", windows, band_matrix, preferred_element_type=jnp.float32)
    return filtered.astype(jnp.bfloat16).reshape(tap_values.shape[0] * row_count, width)


def mixing(weight, coeffs, basis_y, row_count):
    reach = basis_y.shape[1] // 2
    period = jnp.pad(basis_y, ((0, 0), (0, row_count + reach + 1 - basis_y.shape[1])))
    kernel_table = toeplitz(period, row_count)[:, :, reach:]
    kernel_table = kernel_table * (weight * coeffs)[:, None, None]
    return kernel_table.astype(jnp.bfloat16).transpose(1, 0, 2).reshape(row_count, -1)


def pack(strips, owner_table, offset_table, patches):
    strip_count = strips.shape[0]
    fanout = owner_table.shape[1]
    target = owner_table.reshape(-1)
    target_hits = (target[:, None] == jnp.arange(patches, dtype=jnp.int32)[None, :]).astype(
        jnp.int32
    )
    earlier = jnp.cumsum(target_hits, axis=0) - target_hits
    position = jnp.sum(earlier * target_hits, axis=1)
    slot_index = target * CAP + position
    matches = (slot_index[None, :] == jnp.arange(patches * CAP, dtype=jnp.int32)[:, None]).astype(
        jnp.int32
    )
    strip_select = jnp.sum(matches.reshape(patches * CAP, strip_count, fanout), axis=2).astype(
        jnp.bfloat16
    )
    outgoing = jnp.dot(
        strip_select, strips.reshape(strip_count, -1), preferred_element_type=jnp.bfloat16
    )
    filled = jnp.sum(matches, axis=1)
    slot_offset = jnp.sum(matches * offset_table.reshape(-1)[None, :], axis=1) + (filled - 1) * (
        SLAB_ROWS + 8
    )
    return (
        outgoing.reshape(patches, CAP, strips.shape[1], strips.shape[2]),
        slot_offset.reshape(patches, CAP),
    )


def place(received, recv_off, warp_y):
    strip_rows = received.shape[-2]
    width = received.shape[-1]
    starts = recv_off.reshape(-1)
    local_row = jnp.arange(SLAB_ROWS, dtype=jnp.int32)[:, None] - starts[None, :]
    inside = (local_row >= 0) & (local_row < strip_rows)
    tap_index = jnp.arange(strip_rows, dtype=jnp.int32)[None, None, :] - local_row[:, :, None] + 2
    tap_hits = (tap_index[:, :, :, None] == jnp.arange(6, dtype=jnp.int32)).astype(jnp.float32)
    tap_values = jnp.sum(tap_hits * warp_y, axis=3)
    tap_values = (
        jnp.where(inside[:, :, None], tap_values, 0.0).astype(jnp.bfloat16).reshape(SLAB_ROWS, -1)
    )
    return jnp.dot(tap_values, received.reshape(-1, width), preferred_element_type=jnp.float32)


LANE = 128
SPAN = 512


def filter_mix_kernel(slab_ref, halo_ref, band_ref, mix_ref, acc_ref, out_ref):
    full = jnp.concatenate([slab_ref[...], halo_ref[...]], axis=1)
    rows = slab_ref.shape[0]
    blocks = SPAN // LANE
    bases = band_ref.shape[1] // LANE
    windows = jnp.concatenate(
        [full[:, block * LANE : block * LANE + 2 * LANE] for block in range(blocks)], axis=0
    )
    filtered = jnp.dot(windows, band_ref[...], preferred_element_type=jnp.float32)
    filtered = filtered.astype(jnp.bfloat16)
    stacked = jnp.concatenate(
        [
            jnp.concatenate(
                [
                    filtered[block * rows : (block + 1) * rows, base * LANE : (base + 1) * LANE]
                    for block in range(blocks)
                ],
                axis=1,
            )
            for base in range(bases)
        ],
        axis=0,
    )
    out_ref[...] = acc_ref[...] + jnp.dot(mix_ref[...], stacked, preferred_element_type=jnp.float32)


def filter_mix(slab_image, tap_values, mix_matrix, acc):
    rows, width = slab_image.shape
    bases, taps = tap_values.shape
    padded = jnp.pad(slab_image, ((0, 0), (32, SPAN - 32)))
    band_rows = jnp.pad(tap_values, ((0, 0), (15, 2 * LANE + 1 - 15 - taps)))
    band = toeplitz(band_rows, LANE).transpose(2, 0, 1).reshape(2 * LANE, bases * LANE)
    steps = width // SPAN
    return pl.pallas_call(
        filter_mix_kernel,
        grid=(steps,),
        in_specs=[
            pl.BlockSpec((rows, SPAN), lambda k: (0, k)),
            pl.BlockSpec((rows, LANE), lambda k: (0, (k + 1) * (SPAN // LANE))),
            pl.BlockSpec((2 * LANE, bases * LANE), lambda k: (0, 0)),
            pl.BlockSpec((rows, bases * rows), lambda k: (0, 0)),
            pl.BlockSpec((rows, SPAN), lambda k: (0, k)),
        ],
        out_specs=pl.BlockSpec((rows, SPAN), lambda k: (0, k)),
        out_shape=jax.ShapeDtypeStruct((rows, width), jnp.float32),
        input_output_aliases={4: 0},
        cost_estimate=pl.CostEstimate(
            flops=2 * rows * width * 2 * LANE * bases + 2 * rows * width * bases * rows,
            transcendentals=0,
            bytes_accessed=padded.size * 2 + band.size * 2 + mix_matrix.size * 2 + acc.size * 8,
        ),
    )(padded, padded, band, mix_matrix, acc)


def visit_term(received, recv_off, shifts, weight, psf_index, coef_table, basis_x, basis_y, acc):
    warp_x = lanczos_taps(shifts[0])
    warp_y = lanczos_taps(shifts[1])
    slab_image = place(received, recv_off, warp_y).astype(jnp.bfloat16)
    tap_values = combined_taps(basis_x, warp_x).astype(jnp.bfloat16)
    class_hits = (psf_index == jnp.arange(coef_table.shape[0], dtype=jnp.int32)).astype(jnp.float32)
    coeffs = jnp.sum(class_hits[:, None] * coef_table, axis=0)
    mix_matrix = mixing(weight, coeffs, basis_y, SLAB_ROWS)
    return filter_mix(slab_image, tap_values, mix_matrix, acc)


def shards(
    exposures, owners, offsets, visit_shift, visit_weight, psf_class, coef_table, basis_x, basis_y
):
    patches = lax.axis_size("patch")
    streams = lax.axis_size("stream")
    step_count = exposures.shape[0]
    width = exposures.shape[4]
    packed = [
        pack(exposures[step_index, 0], owners[step_index, 0], offsets[step_index, 0], patches)
        for step_index in range(step_count)
    ]
    slot_offsets = jnp.stack([slot_offset for _, slot_offset in packed], axis=1)
    recv_offsets = lax.all_to_all(slot_offsets, "patch", split_axis=0, concat_axis=0, tiled=True)
    outgoing = [strips_out for strips_out, _ in packed]
    received = [None] * step_count
    for step_index in range(min(2, step_count)):
        received[step_index] = lax.all_to_all(
            outgoing[step_index], "patch", split_axis=0, concat_axis=0, tiled=True
        )
    partial_sum = jnp.zeros((SLAB_ROWS, width), jnp.float32)
    for step_index in range(step_count):
        visit_part = visit_term(
            received[step_index],
            recv_offsets[:, step_index],
            visit_shift[step_index, 0],
            visit_weight[step_index, 0],
            psf_class[step_index, 0],
            coef_table,
            basis_x,
            basis_y,
            partial_sum,
        )
        partial_sum = visit_part
        later = step_index + 2
        if later < step_count:
            released, partial_sum = lax.optimization_barrier((outgoing[later], partial_sum))
            received[later] = lax.all_to_all(
                released, "patch", split_axis=0, concat_axis=0, tiled=True
            )
    share_rows = SLAB_ROWS // streams
    pieces = lax.all_to_all(
        partial_sum.reshape(streams, share_rows, width), "stream", split_axis=0, concat_axis=0,
        tiled=True,
    )
    return jnp.sum(pieces, axis=0)


def solution(mesh):
    placed = (
        P(None, "stream", "patch", None, None),
        P(None, "stream", "patch", None),
        P(None, "stream", "patch", None),
        P(None, "stream", None),
        P(None, "stream"),
        P(None, "stream"),
        P(),
        P(),
        P(),
    )
    return jax.shard_map(
        shards, mesh=mesh, in_specs=placed, out_specs=P(("patch", "stream"), None), check_vma=False
    )
```

```python
import jax
import jax.numpy as jnp
from jax import lax
from jax.sharding import Mesh, PartitionSpec as P
from jax.experimental import pallas as pl

CAP = 2
SLAB_ROWS = 64


def lanczos_taps(fraction):
    distance = jnp.arange(6, dtype=jnp.int32).astype(jnp.float32) - 2.0 - fraction
    values = jnp.sinc(distance) * jnp.sinc(distance / 3.0)
    return values / jnp.sum(values)


def combined_taps(basis_rows, warp_x):
    summed = jnp.zeros((basis_rows.shape[0], basis_rows.shape[1] + 5), jnp.float32)
    for tap_slot in range(6):
        summed = summed + jnp.pad(basis_rows * warp_x[tap_slot], ((0, 0), (tap_slot, 5 - tap_slot)))
    return summed


def toeplitz(period, count):
    length = period.shape[-1] - 1
    tiled = jnp.tile(period, [1] * (period.ndim - 1) + [count])
    return tiled[..., : count * length].reshape(period.shape[:-1] + (count, length))


def row_filter(slab_image, tap_values):
    row_count = slab_image.shape[0]
    width = slab_image.shape[1]
    blocks = width // 128
    padded = jnp.pad(slab_image, ((0, 0), (32, 96)))
    front_part = padded[:, :width].reshape(row_count, blocks, 128)
    second = padded[:, 128 : width + 128].reshape(row_count, blocks, 128)[:, :, :64]
    windows = jnp.concatenate([front_part, second], axis=2)
    taps = tap_values.shape[1]
    band_rows = jnp.pad(tap_values, ((0, 0), (15, 193 - 15 - taps)))
    band_matrix = toeplitz(band_rows, 128)
    filtered = jnp.einsum("rna,boa->brno", windows, band_matrix, preferred_element_type=jnp.float32)
    return filtered.astype(jnp.bfloat16).reshape(tap_values.shape[0] * row_count, width)


def mixing(weight, coeffs, basis_y, row_count):
    reach = basis_y.shape[1] // 2
    period = jnp.pad(basis_y, ((0, 0), (0, row_count + reach + 1 - basis_y.shape[1])))
    kernel_table = toeplitz(period, row_count)[:, :, reach:]
    kernel_table = kernel_table * (weight * coeffs)[:, None, None]
    return kernel_table.astype(jnp.bfloat16).transpose(1, 0, 2).reshape(row_count, -1)


def pack(strips, owner_table, offset_table, half, places):
    strip_count = strips.shape[0]
    fanout = owner_table.shape[1]
    owner = owner_table.reshape(-1)
    target = jnp.where(owner % 2 == half, owner // 2, places)
    slots = places + 1
    target_hits = (target[:, None] == jnp.arange(slots, dtype=jnp.int32)[None, :]).astype(jnp.int32)
    earlier = jnp.cumsum(target_hits, axis=0) - target_hits
    position = jnp.sum(earlier * target_hits, axis=1)
    slot_index = target * CAP + position
    matches = (slot_index[None, :] == jnp.arange(places * CAP, dtype=jnp.int32)[:, None]).astype(
        jnp.int32
    )
    strip_select = jnp.sum(matches.reshape(places * CAP, strip_count, fanout), axis=2).astype(
        jnp.bfloat16
    )
    outgoing = jnp.dot(
        strip_select, strips.reshape(strip_count, -1), preferred_element_type=jnp.bfloat16
    )
    filled = jnp.sum(matches, axis=1)
    slot_offset = jnp.sum(matches * offset_table.reshape(-1)[None, :], axis=1) + (filled - 1) * (
        SLAB_ROWS + 8
    )
    return (
        outgoing.reshape(places, CAP, strips.shape[1], strips.shape[2]),
        slot_offset.reshape(places, CAP),
    )


def place(received, recv_off, warp_y):
    strip_rows = received.shape[-2]
    width = received.shape[-1]
    starts = recv_off.reshape(-1)
    local_row = jnp.arange(SLAB_ROWS, dtype=jnp.int32)[:, None] - starts[None, :]
    inside = (local_row >= 0) & (local_row < strip_rows)
    tap_index = jnp.arange(strip_rows, dtype=jnp.int32)[None, None, :] - local_row[:, :, None] + 2
    tap_hits = (tap_index[:, :, :, None] == jnp.arange(6, dtype=jnp.int32)).astype(jnp.float32)
    tap_values = jnp.sum(tap_hits * warp_y, axis=3)
    tap_values = (
        jnp.where(inside[:, :, None], tap_values, 0.0).astype(jnp.bfloat16).reshape(SLAB_ROWS, -1)
    )
    return jnp.dot(tap_values, received.reshape(-1, width), preferred_element_type=jnp.float32)


LANE = 128
SPAN = 512


def filter_mix_kernel(slab_ref, halo_ref, band_ref, mix_ref, acc_ref, out_ref):
    full = jnp.concatenate([slab_ref[...], halo_ref[...]], axis=1)
    rows = slab_ref.shape[0]
    blocks = SPAN // LANE
    bases = band_ref.shape[1] // LANE
    windows = jnp.concatenate(
        [full[:, block * LANE : block * LANE + 2 * LANE] for block in range(blocks)], axis=0
    )
    filtered = jnp.dot(windows, band_ref[...], preferred_element_type=jnp.float32)
    filtered = filtered.astype(jnp.bfloat16)
    stacked = jnp.concatenate(
        [
            jnp.concatenate(
                [
                    filtered[block * rows : (block + 1) * rows, base * LANE : (base + 1) * LANE]
                    for block in range(blocks)
                ],
                axis=1,
            )
            for base in range(bases)
        ],
        axis=0,
    )
    out_ref[...] = acc_ref[...] + jnp.dot(mix_ref[...], stacked, preferred_element_type=jnp.float32)


def filter_mix(slab_image, tap_values, mix_matrix, acc):
    rows, width = slab_image.shape
    bases, taps = tap_values.shape
    padded = jnp.pad(slab_image, ((0, 0), (32, SPAN - 32)))
    band_rows = jnp.pad(tap_values, ((0, 0), (15, 2 * LANE + 1 - 15 - taps)))
    band = toeplitz(band_rows, LANE).transpose(2, 0, 1).reshape(2 * LANE, bases * LANE)
    steps = width // SPAN
    return pl.pallas_call(
        filter_mix_kernel,
        grid=(steps,),
        in_specs=[
            pl.BlockSpec((rows, SPAN), lambda k: (0, k)),
            pl.BlockSpec((rows, LANE), lambda k: (0, (k + 1) * (SPAN // LANE))),
            pl.BlockSpec((2 * LANE, bases * LANE), lambda k: (0, 0)),
            pl.BlockSpec((rows, bases * rows), lambda k: (0, 0)),
            pl.BlockSpec((rows, SPAN), lambda k: (0, k)),
        ],
        out_specs=pl.BlockSpec((rows, SPAN), lambda k: (0, k)),
        out_shape=jax.ShapeDtypeStruct((rows, width), jnp.float32),
        input_output_aliases={4: 0},
        cost_estimate=pl.CostEstimate(
            flops=2 * rows * width * 2 * LANE * bases + 2 * rows * width * bases * rows,
            transcendentals=0,
            bytes_accessed=padded.size * 2 + band.size * 2 + mix_matrix.size * 2 + acc.size * 8,
        ),
    )(padded, padded, band, mix_matrix, acc)


def visit_term(received, recv_off, shifts, weight, psf_index, coef_table, basis_x, basis_y, acc):
    warp_x = lanczos_taps(shifts[0])
    warp_y = lanczos_taps(shifts[1])
    slab_image = place(received, recv_off, warp_y).astype(jnp.bfloat16)
    tap_values = combined_taps(basis_x, warp_x).astype(jnp.bfloat16)
    class_hits = (psf_index == jnp.arange(coef_table.shape[0], dtype=jnp.int32)).astype(jnp.float32)
    coeffs = jnp.sum(class_hits[:, None] * coef_table, axis=0)
    mix_matrix = mixing(weight, coeffs, basis_y, SLAB_ROWS)
    return filter_mix(slab_image, tap_values, mix_matrix, acc)


def cross_half(value, halves, rows):
    mirror = [(h * rows + r, (halves - 1 - h) * rows + rows - 1 - r) for h in range(halves) for r in range(rows)]
    inside = [(h * rows + r, h * rows + rows - 1 - r) for h in range(halves) for r in range(rows)]
    moved = lax.ppermute(value, ("zh", "zl"), mirror)
    return lax.ppermute(moved, ("zh", "zl"), inside)


def shards(
    exposures, owners, offsets, visit_shift, visit_weight, psf_class, coef_table, basis_x, basis_y
):
    places = lax.axis_size(("x", "y"))
    halves = lax.axis_size("zh")
    rows_z = lax.axis_size("zl")
    streams = rows_z * lax.axis_size("c")
    half = lax.axis_index("zh")
    step_count = exposures.shape[0]
    width = exposures.shape[4]
    tables = jnp.stack([owners[:, 0], offsets[:, 0]])
    far_tables = cross_half(tables, halves, rows_z)
    far_strips = [cross_half(exposures[step_index, 0], halves, rows_z) for step_index in range(step_count)]
    own = [
        pack(exposures[step_index, 0], owners[step_index, 0], offsets[step_index, 0], half, places)
        for step_index in range(step_count)
    ]
    far = [
        pack(far_strips[step_index], far_tables[0, step_index], far_tables[1, step_index], half, places)
        for step_index in range(step_count)
    ]
    slot_offsets = jnp.stack(
        [jnp.concatenate([own[t][1], far[t][1]], axis=1) for t in range(step_count)], axis=1
    )
    recv_offsets = lax.all_to_all(slot_offsets, ("x", "y"), split_axis=0, concat_axis=0, tiled=True)
    partial_sum = jnp.zeros((SLAB_ROWS, width), jnp.float32)
    for step_index in range(step_count):
        outgoing = jnp.concatenate([own[step_index][0], far[step_index][0]], axis=1)
        received = lax.all_to_all(outgoing, ("x", "y"), split_axis=0, concat_axis=0, tiled=True)
        partial_sum = visit_term(
            received,
            recv_offsets[:, step_index],
            visit_shift[step_index, 0],
            visit_weight[step_index, 0],
            psf_class[step_index, 0],
            coef_table,
            basis_x,
            basis_y,
            partial_sum,
        )
    share_rows = SLAB_ROWS // streams
    pieces = lax.all_to_all(
        partial_sum.reshape(streams, share_rows, width), ("zl", "c"), split_axis=0, concat_axis=0,
        tiled=True,
    )
    return jnp.sum(pieces, axis=0)


def solution(mesh):
    names = ("x", "y", "zh", "zl", "c")
    patches, streams = mesh.devices.shape
    fine = Mesh(mesh.devices.reshape(4, 4, patches // 16, streams // 2, 2), names)
    patch = ("x", "y", "zh")
    stream = ("zl", "c")
    placed = (
        P(None, stream, patch, None, None),
        P(None, stream, patch, None),
        P(None, stream, patch, None),
        P(None, stream, None),
        P(None, stream),
        P(None, stream),
        P(),
        P(),
        P(),
    )
    return jax.shard_map(
        shards, mesh=fine, in_specs=placed, out_specs=P(patch + stream, None), check_vma=False
    )
```

```python
import jax
import jax.numpy as jnp
from jax import lax
from jax.sharding import Mesh, PartitionSpec as P
from jax.experimental import pallas as pl

CAP = 2
SLAB_ROWS = 64


def lanczos_taps(fraction):
    distance = jnp.arange(6, dtype=jnp.int32).astype(jnp.float32) - 2.0 - fraction
    values = jnp.sinc(distance) * jnp.sinc(distance / 3.0)
    return values / jnp.sum(values)


def combined_taps(basis_rows, warp_x):
    summed = jnp.zeros((basis_rows.shape[0], basis_rows.shape[1] + 5), jnp.float32)
    for tap_slot in range(6):
        summed = summed + jnp.pad(basis_rows * warp_x[tap_slot], ((0, 0), (tap_slot, 5 - tap_slot)))
    return summed


def toeplitz(period, count):
    length = period.shape[-1] - 1
    tiled = jnp.tile(period, [1] * (period.ndim - 1) + [count])
    return tiled[..., : count * length].reshape(period.shape[:-1] + (count, length))


def row_filter(slab_image, tap_values):
    row_count = slab_image.shape[0]
    width = slab_image.shape[1]
    blocks = width // 128
    padded = jnp.pad(slab_image, ((0, 0), (32, 96)))
    front_part = padded[:, :width].reshape(row_count, blocks, 128)
    second = padded[:, 128 : width + 128].reshape(row_count, blocks, 128)[:, :, :64]
    windows = jnp.concatenate([front_part, second], axis=2)
    taps = tap_values.shape[1]
    band_rows = jnp.pad(tap_values, ((0, 0), (15, 193 - 15 - taps)))
    band_matrix = toeplitz(band_rows, 128)
    filtered = jnp.einsum("rna,boa->brno", windows, band_matrix, preferred_element_type=jnp.float32)
    return filtered.astype(jnp.bfloat16).reshape(tap_values.shape[0] * row_count, width)


def mixing(weight, coeffs, basis_y, row_count):
    reach = basis_y.shape[1] // 2
    period = jnp.pad(basis_y, ((0, 0), (0, row_count + reach + 1 - basis_y.shape[1])))
    kernel_table = toeplitz(period, row_count)[:, :, reach:]
    kernel_table = kernel_table * (weight * coeffs)[:, None, None]
    return kernel_table.astype(jnp.bfloat16).transpose(1, 0, 2).reshape(row_count, -1)


def pack(strips, owner_table, offset_table, half, places):
    strip_count = strips.shape[0]
    fanout = owner_table.shape[1]
    owner = owner_table.reshape(-1)
    target = jnp.where(owner % 2 == half, owner // 2, places)
    slots = places + 1
    target_hits = (target[:, None] == jnp.arange(slots, dtype=jnp.int32)[None, :]).astype(jnp.int32)
    earlier = jnp.cumsum(target_hits, axis=0) - target_hits
    position = jnp.sum(earlier * target_hits, axis=1)
    slot_index = target * CAP + position
    matches = (slot_index[None, :] == jnp.arange(places * CAP, dtype=jnp.int32)[:, None]).astype(
        jnp.int32
    )
    strip_select = jnp.sum(matches.reshape(places * CAP, strip_count, fanout), axis=2).astype(
        jnp.bfloat16
    )
    outgoing = jnp.dot(
        strip_select, strips.reshape(strip_count, -1), preferred_element_type=jnp.bfloat16
    )
    filled = jnp.sum(matches, axis=1)
    slot_offset = jnp.sum(matches * offset_table.reshape(-1)[None, :], axis=1) + (filled - 1) * (
        SLAB_ROWS + 8
    )
    return (
        outgoing.reshape(places, CAP, strips.shape[1], strips.shape[2]),
        slot_offset.reshape(places, CAP),
    )


def place(received, recv_off, warp_y):
    strip_rows = received.shape[-2]
    width = received.shape[-1]
    starts = recv_off.reshape(-1)
    local_row = jnp.arange(SLAB_ROWS, dtype=jnp.int32)[:, None] - starts[None, :]
    inside = (local_row >= 0) & (local_row < strip_rows)
    tap_index = jnp.arange(strip_rows, dtype=jnp.int32)[None, None, :] - local_row[:, :, None] + 2
    tap_hits = (tap_index[:, :, :, None] == jnp.arange(6, dtype=jnp.int32)).astype(jnp.float32)
    tap_values = jnp.sum(tap_hits * warp_y, axis=3)
    tap_values = (
        jnp.where(inside[:, :, None], tap_values, 0.0).astype(jnp.bfloat16).reshape(SLAB_ROWS, -1)
    )
    return jnp.dot(tap_values, received.reshape(-1, width), preferred_element_type=jnp.float32)


LANE = 128
SPAN = 512


def filter_mix_kernel(slab_ref, halo_ref, band_ref, mix_ref, acc_ref, out_ref):
    full = jnp.concatenate([slab_ref[...], halo_ref[...]], axis=1)
    rows = slab_ref.shape[0]
    blocks = SPAN // LANE
    bases = band_ref.shape[1] // LANE
    windows = jnp.concatenate(
        [full[:, block * LANE : block * LANE + 2 * LANE] for block in range(blocks)], axis=0
    )
    filtered = jnp.dot(windows, band_ref[...], preferred_element_type=jnp.float32)
    filtered = filtered.astype(jnp.bfloat16)
    stacked = jnp.concatenate(
        [
            jnp.concatenate(
                [
                    filtered[block * rows : (block + 1) * rows, base * LANE : (base + 1) * LANE]
                    for block in range(blocks)
                ],
                axis=1,
            )
            for base in range(bases)
        ],
        axis=0,
    )
    out_ref[...] = acc_ref[...] + jnp.dot(mix_ref[...], stacked, preferred_element_type=jnp.float32)


def filter_mix(slab_image, tap_values, mix_matrix, acc):
    rows, width = slab_image.shape
    bases, taps = tap_values.shape
    padded = jnp.pad(slab_image, ((0, 0), (32, SPAN - 32)))
    band_rows = jnp.pad(tap_values, ((0, 0), (15, 2 * LANE + 1 - 15 - taps)))
    band = toeplitz(band_rows, LANE).transpose(2, 0, 1).reshape(2 * LANE, bases * LANE)
    steps = width // SPAN
    return pl.pallas_call(
        filter_mix_kernel,
        grid=(steps,),
        in_specs=[
            pl.BlockSpec((rows, SPAN), lambda k: (0, k)),
            pl.BlockSpec((rows, LANE), lambda k: (0, (k + 1) * (SPAN // LANE))),
            pl.BlockSpec((2 * LANE, bases * LANE), lambda k: (0, 0)),
            pl.BlockSpec((rows, bases * rows), lambda k: (0, 0)),
            pl.BlockSpec((rows, SPAN), lambda k: (0, k)),
        ],
        out_specs=pl.BlockSpec((rows, SPAN), lambda k: (0, k)),
        out_shape=jax.ShapeDtypeStruct((rows, width), jnp.float32),
        input_output_aliases={4: 0},
        cost_estimate=pl.CostEstimate(
            flops=2 * rows * width * 2 * LANE * bases + 2 * rows * width * bases * rows,
            transcendentals=0,
            bytes_accessed=padded.size * 2 + band.size * 2 + mix_matrix.size * 2 + acc.size * 8,
        ),
    )(padded, padded, band, mix_matrix, acc)


def visit_term(received, recv_off, shifts, weight, psf_index, coef_table, basis_x, basis_y, acc):
    warp_x = lanczos_taps(shifts[0])
    warp_y = lanczos_taps(shifts[1])
    slab_image = place(received, recv_off, warp_y).astype(jnp.bfloat16)
    tap_values = combined_taps(basis_x, warp_x).astype(jnp.bfloat16)
    class_hits = (psf_index == jnp.arange(coef_table.shape[0], dtype=jnp.int32)).astype(jnp.float32)
    coeffs = jnp.sum(class_hits[:, None] * coef_table, axis=0)
    mix_matrix = mixing(weight, coeffs, basis_y, SLAB_ROWS)
    return filter_mix(slab_image, tap_values, mix_matrix, acc)


def cross_half(value, halves, rows):
    mirror = [(h * rows + r, (halves - 1 - h) * rows + rows - 1 - r) for h in range(halves) for r in range(rows)]
    inside = [(h * rows + r, h * rows + rows - 1 - r) for h in range(halves) for r in range(rows)]
    moved = lax.ppermute(value, ("zh", "zl"), mirror)
    return lax.ppermute(moved, ("zh", "zl"), inside)


def shards(
    exposures, owners, offsets, visit_shift, visit_weight, psf_class, coef_table, basis_x, basis_y
):
    places = lax.axis_size(("x", "y"))
    halves = lax.axis_size("zh")
    rows_z = lax.axis_size("zl")
    streams = rows_z * lax.axis_size("c")
    half = lax.axis_index("zh")
    step_count = exposures.shape[0]
    width = exposures.shape[4]
    strip_rows = exposures.shape[3]
    fanout = owners.shape[3]
    strip_count = exposures.shape[2]
    table = jnp.concatenate([owners[:, 0], offsets[:, 0]], axis=2).reshape(-1)
    table_strip = jnp.zeros((1, strip_rows, width), exposures.dtype)
    table_strip = table_strip.at[0, 0, : table.shape[0]].set(table.astype(exposures.dtype))
    far_strips = []
    for step_index in range(step_count):
        strips = exposures[step_index, 0]
        if step_index == 0:
            strips = jnp.concatenate([strips, table_strip], axis=0)
        far_strips.append(cross_half(strips, halves, rows_z))
    far_table = far_strips[0][strip_count, 0, : table.shape[0]].astype(jnp.int32)
    far_table = far_table.reshape(step_count, strip_count, 2 * fanout)
    own = [
        pack(exposures[step_index, 0], owners[step_index, 0], offsets[step_index, 0], half, places)
        for step_index in range(step_count)
    ]
    far = [
        pack(
            far_strips[step_index][:strip_count],
            far_table[step_index, :, :fanout],
            far_table[step_index, :, fanout:],
            half,
            places,
        )
        for step_index in range(step_count)
    ]
    slot_offsets = jnp.stack(
        [jnp.concatenate([own[t][1], far[t][1]], axis=1) for t in range(step_count)], axis=1
    )
    recv_offsets = lax.all_to_all(slot_offsets, ("x", "y"), split_axis=0, concat_axis=0, tiled=True)
    outgoing = [
        jnp.concatenate([own[step_index][0], far[step_index][0]], axis=1)
        for step_index in range(step_count)
    ]
    received = [None] * step_count
    for step_index in range(min(2, step_count)):
        received[step_index] = lax.all_to_all(
            outgoing[step_index], ("x", "y"), split_axis=0, concat_axis=0, tiled=True
        )
    partial_sum = jnp.zeros((SLAB_ROWS, width), jnp.float32)
    for step_index in range(step_count):
        partial_sum = visit_term(
            received[step_index],
            recv_offsets[:, step_index],
            visit_shift[step_index, 0],
            visit_weight[step_index, 0],
            psf_class[step_index, 0],
            coef_table,
            basis_x,
            basis_y,
            partial_sum,
        )
        later = step_index + 2
        if later < step_count:
            released, partial_sum = lax.optimization_barrier((outgoing[later], partial_sum))
            received[later] = lax.all_to_all(
                released, ("x", "y"), split_axis=0, concat_axis=0, tiled=True
            )
    share_rows = SLAB_ROWS // streams
    pieces = lax.all_to_all(
        partial_sum.reshape(streams, share_rows, width), ("zl", "c"), split_axis=0, concat_axis=0,
        tiled=True,
    )
    return jnp.sum(pieces, axis=0)


def solution(mesh):
    names = ("x", "y", "zh", "zl", "c")
    patches, streams = mesh.devices.shape
    fine = Mesh(mesh.devices.reshape(4, 4, patches // 16, streams // 2, 2), names)
    patch = ("x", "y", "zh")
    stream = ("zl", "c")
    placed = (
        P(None, stream, patch, None, None),
        P(None, stream, patch, None),
        P(None, stream, patch, None),
        P(None, stream, None),
        P(None, stream),
        P(None, stream),
        P(),
        P(),
        P(),
    )
    return jax.shard_map(
        shards, mesh=fine, in_specs=placed, out_specs=P(patch + stream, None), check_vma=False
    )
```

```python
import jax
import jax.numpy as jnp
from jax import lax
from jax.sharding import Mesh, PartitionSpec as P
from jax.experimental import pallas as pl

CAP = 2
SLAB_ROWS = 64


def lanczos_taps(fraction):
    distance = jnp.arange(6, dtype=jnp.int32).astype(jnp.float32) - 2.0 - fraction
    values = jnp.sinc(distance) * jnp.sinc(distance / 3.0)
    return values / jnp.sum(values)


def combined_taps(basis_rows, warp_x):
    summed = jnp.zeros((basis_rows.shape[0], basis_rows.shape[1] + 5), jnp.float32)
    for tap_slot in range(6):
        summed = summed + jnp.pad(basis_rows * warp_x[tap_slot], ((0, 0), (tap_slot, 5 - tap_slot)))
    return summed


def toeplitz(period, count):
    length = period.shape[-1] - 1
    tiled = jnp.tile(period, [1] * (period.ndim - 1) + [count])
    return tiled[..., : count * length].reshape(period.shape[:-1] + (count, length))


def row_filter(slab_image, tap_values):
    row_count = slab_image.shape[0]
    width = slab_image.shape[1]
    blocks = width // 128
    padded = jnp.pad(slab_image, ((0, 0), (32, 96)))
    front_part = padded[:, :width].reshape(row_count, blocks, 128)
    second = padded[:, 128 : width + 128].reshape(row_count, blocks, 128)[:, :, :64]
    windows = jnp.concatenate([front_part, second], axis=2)
    taps = tap_values.shape[1]
    band_rows = jnp.pad(tap_values, ((0, 0), (15, 193 - 15 - taps)))
    band_matrix = toeplitz(band_rows, 128)
    filtered = jnp.einsum("rna,boa->brno", windows, band_matrix, preferred_element_type=jnp.float32)
    return filtered.astype(jnp.bfloat16).reshape(tap_values.shape[0] * row_count, width)


def mixing(weight, coeffs, basis_y, row_count):
    reach = basis_y.shape[1] // 2
    period = jnp.pad(basis_y, ((0, 0), (0, row_count + reach + 1 - basis_y.shape[1])))
    kernel_table = toeplitz(period, row_count)[:, :, reach:]
    kernel_table = kernel_table * (weight * coeffs)[:, None, None]
    return kernel_table.astype(jnp.bfloat16).transpose(1, 0, 2).reshape(row_count, -1)


def pack(strips, owner_table, offset_table, half, places):
    strip_count = strips.shape[0]
    fanout = owner_table.shape[1]
    owner = owner_table.reshape(-1)
    target = jnp.where(owner % 2 == half, owner // 2, places)
    slots = places + 1
    target_hits = (target[:, None] == jnp.arange(slots, dtype=jnp.int32)[None, :]).astype(jnp.int32)
    earlier = jnp.cumsum(target_hits, axis=0) - target_hits
    position = jnp.sum(earlier * target_hits, axis=1)
    slot_index = target * CAP + position
    matches = (slot_index[None, :] == jnp.arange(places * CAP, dtype=jnp.int32)[:, None]).astype(
        jnp.int32
    )
    strip_select = jnp.sum(matches.reshape(places * CAP, strip_count, fanout), axis=2).astype(
        jnp.bfloat16
    )
    outgoing = jnp.dot(
        strip_select, strips.reshape(strip_count, -1), preferred_element_type=jnp.bfloat16
    )
    filled = jnp.sum(matches, axis=1)
    slot_offset = jnp.sum(matches * offset_table.reshape(-1)[None, :], axis=1) + (filled - 1) * (
        SLAB_ROWS + 8
    )
    return (
        outgoing.reshape(places, CAP, strips.shape[1], strips.shape[2]),
        slot_offset.reshape(places, CAP),
    )


def place(received, recv_off, warp_y):
    strip_rows = received.shape[-2]
    width = received.shape[-1]
    starts = recv_off.reshape(-1)
    local_row = jnp.arange(SLAB_ROWS, dtype=jnp.int32)[:, None] - starts[None, :]
    inside = (local_row >= 0) & (local_row < strip_rows)
    tap_index = jnp.arange(strip_rows, dtype=jnp.int32)[None, None, :] - local_row[:, :, None] + 2
    tap_hits = (tap_index[:, :, :, None] == jnp.arange(6, dtype=jnp.int32)).astype(jnp.float32)
    tap_values = jnp.sum(tap_hits * warp_y, axis=3)
    tap_values = (
        jnp.where(inside[:, :, None], tap_values, 0.0).astype(jnp.bfloat16).reshape(SLAB_ROWS, -1)
    )
    return jnp.dot(tap_values, received.reshape(-1, width), preferred_element_type=jnp.float32)


LANE = 128
SPAN = 512


def filter_mix_kernel(slab_ref, halo_ref, band_ref, mix_ref, acc_ref, out_ref):
    full = jnp.concatenate([slab_ref[...], halo_ref[...]], axis=1)
    rows = slab_ref.shape[0]
    blocks = SPAN // LANE
    bases = band_ref.shape[1] // LANE
    windows = jnp.concatenate(
        [full[:, block * LANE : block * LANE + 2 * LANE] for block in range(blocks)], axis=0
    )
    filtered = jnp.dot(windows, band_ref[...], preferred_element_type=jnp.float32)
    filtered = filtered.astype(jnp.bfloat16)
    stacked = jnp.concatenate(
        [
            jnp.concatenate(
                [
                    filtered[block * rows : (block + 1) * rows, base * LANE : (base + 1) * LANE]
                    for block in range(blocks)
                ],
                axis=1,
            )
            for base in range(bases)
        ],
        axis=0,
    )
    out_ref[...] = acc_ref[...] + jnp.dot(mix_ref[...], stacked, preferred_element_type=jnp.float32)


def filter_mix(slab_image, tap_values, mix_matrix, acc):
    rows, width = slab_image.shape
    bases, taps = tap_values.shape
    padded = jnp.pad(slab_image, ((0, 0), (32, SPAN - 32)))
    band_rows = jnp.pad(tap_values, ((0, 0), (15, 2 * LANE + 1 - 15 - taps)))
    band = toeplitz(band_rows, LANE).transpose(2, 0, 1).reshape(2 * LANE, bases * LANE)
    steps = width // SPAN
    return pl.pallas_call(
        filter_mix_kernel,
        grid=(steps,),
        in_specs=[
            pl.BlockSpec((rows, SPAN), lambda k: (0, k)),
            pl.BlockSpec((rows, LANE), lambda k: (0, (k + 1) * (SPAN // LANE))),
            pl.BlockSpec((2 * LANE, bases * LANE), lambda k: (0, 0)),
            pl.BlockSpec((rows, bases * rows), lambda k: (0, 0)),
            pl.BlockSpec((rows, SPAN), lambda k: (0, k)),
        ],
        out_specs=pl.BlockSpec((rows, SPAN), lambda k: (0, k)),
        out_shape=jax.ShapeDtypeStruct((rows, width), jnp.float32),
        input_output_aliases={4: 0},
        cost_estimate=pl.CostEstimate(
            flops=2 * rows * width * 2 * LANE * bases + 2 * rows * width * bases * rows,
            transcendentals=0,
            bytes_accessed=padded.size * 2 + band.size * 2 + mix_matrix.size * 2 + acc.size * 8,
        ),
    )(padded, padded, band, mix_matrix, acc)


def visit_term(received, recv_off, shifts, weight, psf_index, coef_table, basis_x, basis_y, acc):
    warp_x = lanczos_taps(shifts[0])
    warp_y = lanczos_taps(shifts[1])
    slab_image = place(received, recv_off, warp_y).astype(jnp.bfloat16)
    tap_values = combined_taps(basis_x, warp_x).astype(jnp.bfloat16)
    class_hits = (psf_index == jnp.arange(coef_table.shape[0], dtype=jnp.int32)).astype(jnp.float32)
    coeffs = jnp.sum(class_hits[:, None] * coef_table, axis=0)
    mix_matrix = mixing(weight, coeffs, basis_y, SLAB_ROWS)
    return filter_mix(slab_image, tap_values, mix_matrix, acc)


def mirror_pairs(halves, rows):
    return [(h * rows + r, (halves - 1 - h) * rows + rows - 1 - r) for h in range(halves) for r in range(rows)]


def inside_pairs(halves, rows):
    return [(h * rows + r, h * rows + rows - 1 - r) for h in range(halves) for r in range(rows)]


def shards(
    exposures, owners, offsets, visit_shift, visit_weight, psf_class, coef_table, basis_x, basis_y
):
    places = lax.axis_size(("x", "y"))
    halves = lax.axis_size("zh")
    rows_z = lax.axis_size("zl")
    streams = rows_z * lax.axis_size("c")
    half = lax.axis_index("zh")
    step_count = exposures.shape[0]
    width = exposures.shape[4]
    strip_rows = exposures.shape[3]
    fanout = owners.shape[3]
    strip_count = exposures.shape[2]
    table = jnp.concatenate([owners[:, 0], offsets[:, 0]], axis=2).reshape(-1)
    table_strip = jnp.zeros((1, strip_rows, width), exposures.dtype)
    table_strip = table_strip.at[0, 0, : table.shape[0]].set(table.astype(exposures.dtype))
    far_strips = []
    landed = None
    for step_index in range(step_count):
        strips = exposures[step_index, 0]
        if step_index == 0:
            strips = jnp.concatenate([strips, table_strip], axis=0)
        else:
            strips, _ = lax.optimization_barrier((strips, landed))
        landed = lax.ppermute(strips, ("zh", "zl"), mirror_pairs(halves, rows_z))
        far_strips.append(lax.ppermute(landed, ("zh", "zl"), inside_pairs(halves, rows_z)))
    far_table = far_strips[0][strip_count, 0, : table.shape[0]].astype(jnp.int32)
    far_table = far_table.reshape(step_count, strip_count, 2 * fanout)
    own = [
        pack(exposures[step_index, 0], owners[step_index, 0], offsets[step_index, 0], half, places)
        for step_index in range(step_count)
    ]
    far = [
        pack(
            far_strips[step_index][:strip_count],
            far_table[step_index, :, :fanout],
            far_table[step_index, :, fanout:],
            half,
            places,
        )
        for step_index in range(step_count)
    ]
    slot_offsets = jnp.stack(
        [jnp.concatenate([own[t][1], far[t][1]], axis=1) for t in range(step_count)], axis=1
    )
    recv_offsets = lax.all_to_all(slot_offsets, ("x", "y"), split_axis=0, concat_axis=0, tiled=True)
    outgoing = [
        jnp.concatenate([own[step_index][0], far[step_index][0]], axis=1)
        for step_index in range(step_count)
    ]
    received = [None] * step_count
    for step_index in range(min(2, step_count)):
        received[step_index] = lax.all_to_all(
            outgoing[step_index], ("x", "y"), split_axis=0, concat_axis=0, tiled=True
        )
    partial_sum = jnp.zeros((SLAB_ROWS, width), jnp.float32)
    for step_index in range(step_count):
        partial_sum = visit_term(
            received[step_index],
            recv_offsets[:, step_index],
            visit_shift[step_index, 0],
            visit_weight[step_index, 0],
            psf_class[step_index, 0],
            coef_table,
            basis_x,
            basis_y,
            partial_sum,
        )
        later = step_index + 2
        if later < step_count:
            released, partial_sum = lax.optimization_barrier((outgoing[later], partial_sum))
            received[later] = lax.all_to_all(
                released, ("x", "y"), split_axis=0, concat_axis=0, tiled=True
            )
    share_rows = SLAB_ROWS // streams
    pieces = lax.all_to_all(
        partial_sum.reshape(streams, share_rows, width), ("zl", "c"), split_axis=0, concat_axis=0,
        tiled=True,
    )
    return jnp.sum(pieces, axis=0)


def solution(mesh):
    names = ("x", "y", "zh", "zl", "c")
    patches, streams = mesh.devices.shape
    fine = Mesh(mesh.devices.reshape(4, 4, patches // 16, streams // 2, 2), names)
    patch = ("x", "y", "zh")
    stream = ("zl", "c")
    placed = (
        P(None, stream, patch, None, None),
        P(None, stream, patch, None),
        P(None, stream, patch, None),
        P(None, stream, None),
        P(None, stream),
        P(None, stream),
        P(),
        P(),
        P(),
    )
    return jax.shard_map(
        shards, mesh=fine, in_specs=placed, out_specs=P(patch + stream, None), check_vma=False
    )
```

```python
import jax
import jax.numpy as jnp
from jax import lax
from jax.sharding import Mesh, PartitionSpec as P
from jax.experimental import pallas as pl

CAP = 2
SLAB_ROWS = 64


def lanczos_taps(fraction):
    distance = jnp.arange(6, dtype=jnp.int32).astype(jnp.float32) - 2.0 - fraction
    values = jnp.sinc(distance) * jnp.sinc(distance / 3.0)
    return values / jnp.sum(values)


def combined_taps(basis_rows, warp_x):
    summed = jnp.zeros((basis_rows.shape[0], basis_rows.shape[1] + 5), jnp.float32)
    for tap_slot in range(6):
        summed = summed + jnp.pad(basis_rows * warp_x[tap_slot], ((0, 0), (tap_slot, 5 - tap_slot)))
    return summed


def toeplitz(period, count):
    length = period.shape[-1] - 1
    tiled = jnp.tile(period, [1] * (period.ndim - 1) + [count])
    return tiled[..., : count * length].reshape(period.shape[:-1] + (count, length))


def row_filter(slab_image, tap_values):
    row_count = slab_image.shape[0]
    width = slab_image.shape[1]
    blocks = width // 128
    padded = jnp.pad(slab_image, ((0, 0), (32, 96)))
    front_part = padded[:, :width].reshape(row_count, blocks, 128)
    second = padded[:, 128 : width + 128].reshape(row_count, blocks, 128)[:, :, :64]
    windows = jnp.concatenate([front_part, second], axis=2)
    taps = tap_values.shape[1]
    band_rows = jnp.pad(tap_values, ((0, 0), (15, 193 - 15 - taps)))
    band_matrix = toeplitz(band_rows, 128)
    filtered = jnp.einsum("rna,boa->brno", windows, band_matrix, preferred_element_type=jnp.float32)
    return filtered.astype(jnp.bfloat16).reshape(tap_values.shape[0] * row_count, width)


def mixing(weight, coeffs, basis_y, row_count):
    reach = basis_y.shape[1] // 2
    period = jnp.pad(basis_y, ((0, 0), (0, row_count + reach + 1 - basis_y.shape[1])))
    kernel_table = toeplitz(period, row_count)[:, :, reach:]
    kernel_table = kernel_table * (weight * coeffs)[:, None, None]
    return kernel_table.astype(jnp.bfloat16).transpose(1, 0, 2).reshape(row_count, -1)


def pack(strips, owner_table, offset_table, half, places):
    strip_count = strips.shape[0]
    fanout = owner_table.shape[1]
    owner = owner_table.reshape(-1)
    target = jnp.where(owner % 2 == half, owner // 2, places)
    slots = places + 1
    target_hits = (target[:, None] == jnp.arange(slots, dtype=jnp.int32)[None, :]).astype(jnp.int32)
    earlier = jnp.cumsum(target_hits, axis=0) - target_hits
    position = jnp.sum(earlier * target_hits, axis=1)
    slot_index = target * CAP + position
    matches = (slot_index[None, :] == jnp.arange(places * CAP, dtype=jnp.int32)[:, None]).astype(
        jnp.int32
    )
    strip_select = jnp.sum(matches.reshape(places * CAP, strip_count, fanout), axis=2).astype(
        jnp.bfloat16
    )
    outgoing = jnp.dot(
        strip_select, strips.reshape(strip_count, -1), preferred_element_type=jnp.bfloat16
    )
    filled = jnp.sum(matches, axis=1)
    slot_offset = jnp.sum(matches * offset_table.reshape(-1)[None, :], axis=1) + (filled - 1) * (
        SLAB_ROWS + 8
    )
    return (
        outgoing.reshape(places, CAP, strips.shape[1], strips.shape[2]),
        slot_offset.reshape(places, CAP),
    )


def place(received, recv_off, warp_y):
    strip_rows = received.shape[-2]
    width = received.shape[-1]
    starts = recv_off.reshape(-1)
    local_row = jnp.arange(SLAB_ROWS, dtype=jnp.int32)[:, None] - starts[None, :]
    inside = (local_row >= 0) & (local_row < strip_rows)
    tap_index = jnp.arange(strip_rows, dtype=jnp.int32)[None, None, :] - local_row[:, :, None] + 2
    tap_hits = (tap_index[:, :, :, None] == jnp.arange(6, dtype=jnp.int32)).astype(jnp.float32)
    tap_values = jnp.sum(tap_hits * warp_y, axis=3)
    tap_values = (
        jnp.where(inside[:, :, None], tap_values, 0.0).astype(jnp.bfloat16).reshape(SLAB_ROWS, -1)
    )
    return jnp.dot(tap_values, received.reshape(-1, width), preferred_element_type=jnp.float32)


LANE = 128
SPAN = 512


def filter_mix_kernel(slab_ref, halo_ref, band_ref, mix_ref, acc_ref, out_ref):
    full = jnp.concatenate([slab_ref[...], halo_ref[...]], axis=1)
    rows = slab_ref.shape[0]
    blocks = SPAN // LANE
    bases = band_ref.shape[1] // LANE
    windows = jnp.concatenate(
        [full[:, block * LANE : block * LANE + 2 * LANE] for block in range(blocks)], axis=0
    )
    filtered = jnp.dot(windows, band_ref[...], preferred_element_type=jnp.float32)
    filtered = filtered.astype(jnp.bfloat16)
    stacked = jnp.concatenate(
        [
            jnp.concatenate(
                [
                    filtered[block * rows : (block + 1) * rows, base * LANE : (base + 1) * LANE]
                    for block in range(blocks)
                ],
                axis=1,
            )
            for base in range(bases)
        ],
        axis=0,
    )
    out_ref[...] = acc_ref[...] + jnp.dot(mix_ref[...], stacked, preferred_element_type=jnp.float32)


def filter_mix(slab_image, tap_values, mix_matrix, acc):
    rows, width = slab_image.shape
    bases, taps = tap_values.shape
    padded = jnp.pad(slab_image, ((0, 0), (32, SPAN - 32)))
    band_rows = jnp.pad(tap_values, ((0, 0), (15, 2 * LANE + 1 - 15 - taps)))
    band = toeplitz(band_rows, LANE).transpose(2, 0, 1).reshape(2 * LANE, bases * LANE)
    steps = width // SPAN
    return pl.pallas_call(
        filter_mix_kernel,
        grid=(steps,),
        in_specs=[
            pl.BlockSpec((rows, SPAN), lambda k: (0, k)),
            pl.BlockSpec((rows, LANE), lambda k: (0, (k + 1) * (SPAN // LANE))),
            pl.BlockSpec((2 * LANE, bases * LANE), lambda k: (0, 0)),
            pl.BlockSpec((rows, bases * rows), lambda k: (0, 0)),
            pl.BlockSpec((rows, SPAN), lambda k: (0, k)),
        ],
        out_specs=pl.BlockSpec((rows, SPAN), lambda k: (0, k)),
        out_shape=jax.ShapeDtypeStruct((rows, width), jnp.float32),
        input_output_aliases={4: 0},
        cost_estimate=pl.CostEstimate(
            flops=2 * rows * width * 2 * LANE * bases + 2 * rows * width * bases * rows,
            transcendentals=0,
            bytes_accessed=padded.size * 2 + band.size * 2 + mix_matrix.size * 2 + acc.size * 8,
        ),
    )(padded, padded, band, mix_matrix, acc)


def visit_term(received, recv_off, shifts, weight, psf_index, coef_table, basis_x, basis_y, acc):
    warp_x = lanczos_taps(shifts[0])
    warp_y = lanczos_taps(shifts[1])
    slab_image = place(received, recv_off, warp_y).astype(jnp.bfloat16)
    tap_values = combined_taps(basis_x, warp_x).astype(jnp.bfloat16)
    class_hits = (psf_index == jnp.arange(coef_table.shape[0], dtype=jnp.int32)).astype(jnp.float32)
    coeffs = jnp.sum(class_hits[:, None] * coef_table, axis=0)
    mix_matrix = mixing(weight, coeffs, basis_y, SLAB_ROWS)
    return filter_mix(slab_image, tap_values, mix_matrix, acc)


def across_pairs(halves, rows):
    return [(h * rows + r, (halves - 1 - h) * rows + r) for h in range(halves) for r in range(rows)]


def shards(
    exposures, owners, offsets, visit_shift, visit_weight, psf_class, coef_table, basis_x, basis_y
):
    places = lax.axis_size(("x", "y"))
    halves = lax.axis_size("zh")
    rows_z = lax.axis_size("zl")
    streams = rows_z * lax.axis_size("c")
    half = lax.axis_index("zh")
    step_count = exposures.shape[0]
    width = exposures.shape[4]
    strip_rows = exposures.shape[3]
    fanout = owners.shape[3]
    strip_count = exposures.shape[2]
    table = jnp.concatenate([owners[:, 0], offsets[:, 0]], axis=2).reshape(-1)
    table_strip = jnp.zeros((1, strip_rows, width), exposures.dtype)
    table_strip = table_strip.at[0, 0, : table.shape[0]].set(table.astype(exposures.dtype))
    far_strips = []
    landed = None
    for step_index in range(step_count):
        strips = exposures[step_index, 0]
        if step_index == 0:
            strips = jnp.concatenate([strips, table_strip], axis=0)
        else:
            strips, _ = lax.optimization_barrier((strips, landed))
        landed = lax.ppermute(strips, ("zh", "zl"), across_pairs(halves, rows_z))
        far_strips.append(landed)
    far_table = far_strips[0][strip_count, 0, : table.shape[0]].astype(jnp.int32)
    far_table = far_table.reshape(step_count, strip_count, 2 * fanout)
    own = [
        pack(exposures[step_index, 0], owners[step_index, 0], offsets[step_index, 0], half, places)
        for step_index in range(step_count)
    ]
    far = [
        pack(
            far_strips[step_index][:strip_count],
            far_table[step_index, :, :fanout],
            far_table[step_index, :, fanout:],
            half,
            places,
        )
        for step_index in range(step_count)
    ]
    slot_offsets = jnp.stack(
        [jnp.concatenate([own[t][1], far[t][1]], axis=1) for t in range(step_count)], axis=1
    )
    recv_offsets = lax.all_to_all(slot_offsets, ("x", "y"), split_axis=0, concat_axis=0, tiled=True)
    outgoing = [
        jnp.concatenate([own[step_index][0], far[step_index][0]], axis=1)
        for step_index in range(step_count)
    ]
    received = [None] * step_count
    for step_index in range(min(2, step_count)):
        received[step_index] = lax.all_to_all(
            outgoing[step_index], ("x", "y"), split_axis=0, concat_axis=0, tiled=True
        )
    partial_sum = jnp.zeros((SLAB_ROWS, width), jnp.float32)
    for step_index in range(step_count):
        partial_sum = visit_term(
            received[step_index],
            recv_offsets[:, step_index],
            visit_shift[step_index, 0],
            visit_weight[step_index, 0],
            psf_class[step_index, 0],
            coef_table,
            basis_x,
            basis_y,
            partial_sum,
        )
        later = step_index + 2
        if later < step_count:
            released, partial_sum = lax.optimization_barrier((outgoing[later], partial_sum))
            received[later] = lax.all_to_all(
                released, ("x", "y"), split_axis=0, concat_axis=0, tiled=True
            )
    share_rows = SLAB_ROWS // streams
    pieces = lax.all_to_all(
        partial_sum.reshape(streams, share_rows, width), ("zl", "c"), split_axis=0, concat_axis=0,
        tiled=True,
    )
    return jnp.sum(pieces, axis=0)


def solution(mesh):
    names = ("x", "y", "zh", "zl", "c")
    patches, streams = mesh.devices.shape
    fine = Mesh(mesh.devices.reshape(4, 4, patches // 16, streams // 2, 2), names)
    patch = ("x", "y", "zh")
    stream = ("zl", "c")
    placed = (
        P(None, stream, patch, None, None),
        P(None, stream, patch, None),
        P(None, stream, patch, None),
        P(None, stream, None),
        P(None, stream),
        P(None, stream),
        P(),
        P(),
        P(),
    )
    return jax.shard_map(
        shards, mesh=fine, in_specs=placed, out_specs=P(patch + stream, None), check_vma=False
    )
```

```python
import jax
import jax.numpy as jnp
from jax import lax
from jax.sharding import Mesh, PartitionSpec as P
from jax.experimental import pallas as pl

CAP = 2
SLAB_ROWS = 64


def lanczos_taps(fraction):
    distance = jnp.arange(6, dtype=jnp.int32).astype(jnp.float32) - 2.0 - fraction
    values = jnp.sinc(distance) * jnp.sinc(distance / 3.0)
    return values / jnp.sum(values)


def combined_taps(basis_rows, warp_x):
    summed = jnp.zeros((basis_rows.shape[0], basis_rows.shape[1] + 5), jnp.float32)
    for tap_slot in range(6):
        summed = summed + jnp.pad(basis_rows * warp_x[tap_slot], ((0, 0), (tap_slot, 5 - tap_slot)))
    return summed


def toeplitz(period, count):
    length = period.shape[-1] - 1
    tiled = jnp.tile(period, [1] * (period.ndim - 1) + [count])
    return tiled[..., : count * length].reshape(period.shape[:-1] + (count, length))


def row_filter(slab_image, tap_values):
    row_count = slab_image.shape[0]
    width = slab_image.shape[1]
    blocks = width // 128
    padded = jnp.pad(slab_image, ((0, 0), (32, 96)))
    front_part = padded[:, :width].reshape(row_count, blocks, 128)
    second = padded[:, 128 : width + 128].reshape(row_count, blocks, 128)[:, :, :64]
    windows = jnp.concatenate([front_part, second], axis=2)
    taps = tap_values.shape[1]
    band_rows = jnp.pad(tap_values, ((0, 0), (15, 193 - 15 - taps)))
    band_matrix = toeplitz(band_rows, 128)
    filtered = jnp.einsum("rna,boa->brno", windows, band_matrix, preferred_element_type=jnp.float32)
    return filtered.astype(jnp.bfloat16).reshape(tap_values.shape[0] * row_count, width)


def mixing(weight, coeffs, basis_y, row_count):
    reach = basis_y.shape[1] // 2
    period = jnp.pad(basis_y, ((0, 0), (0, row_count + reach + 1 - basis_y.shape[1])))
    kernel_table = toeplitz(period, row_count)[:, :, reach:]
    kernel_table = kernel_table * (weight * coeffs)[:, None, None]
    return kernel_table.astype(jnp.bfloat16).transpose(1, 0, 2).reshape(row_count, -1)


def pack(strips, owner_table, offset_table, half, places):
    strip_count = strips.shape[0]
    fanout = owner_table.shape[1]
    owner = owner_table.reshape(-1)
    target = jnp.where(owner % 2 == half, owner // 2, places)
    slots = places + 1
    target_hits = (target[:, None] == jnp.arange(slots, dtype=jnp.int32)[None, :]).astype(jnp.int32)
    earlier = jnp.cumsum(target_hits, axis=0) - target_hits
    position = jnp.sum(earlier * target_hits, axis=1)
    slot_index = target * CAP + position
    matches = (slot_index[None, :] == jnp.arange(places * CAP, dtype=jnp.int32)[:, None]).astype(
        jnp.int32
    )
    strip_select = jnp.sum(matches.reshape(places * CAP, strip_count, fanout), axis=2).astype(
        jnp.bfloat16
    )
    outgoing = jnp.dot(
        strip_select, strips.reshape(strip_count, -1), preferred_element_type=jnp.bfloat16
    )
    filled = jnp.sum(matches, axis=1)
    slot_offset = jnp.sum(matches * offset_table.reshape(-1)[None, :], axis=1) + (filled - 1) * (
        SLAB_ROWS + 8
    )
    return (
        outgoing.reshape(places, CAP, strips.shape[1], strips.shape[2]),
        slot_offset.reshape(places, CAP),
    )


def place(received, recv_off, warp_y):
    strip_rows = received.shape[-2]
    width = received.shape[-1]
    starts = recv_off.reshape(-1)
    local_row = jnp.arange(SLAB_ROWS, dtype=jnp.int32)[:, None] - starts[None, :]
    inside = (local_row >= 0) & (local_row < strip_rows)
    tap_index = jnp.arange(strip_rows, dtype=jnp.int32)[None, None, :] - local_row[:, :, None] + 2
    tap_hits = (tap_index[:, :, :, None] == jnp.arange(6, dtype=jnp.int32)).astype(jnp.float32)
    tap_values = jnp.sum(tap_hits * warp_y, axis=3)
    tap_values = (
        jnp.where(inside[:, :, None], tap_values, 0.0).astype(jnp.bfloat16).reshape(SLAB_ROWS, -1)
    )
    return jnp.dot(tap_values, received.reshape(-1, width), preferred_element_type=jnp.float32)


LANE = 128
SPAN = 512


def filter_mix_kernel(slab_ref, halo_ref, band_ref, mix_ref, acc_ref, out_ref):
    full = jnp.concatenate([slab_ref[...], halo_ref[...]], axis=1)
    rows = slab_ref.shape[0]
    blocks = SPAN // LANE
    bases = band_ref.shape[1] // LANE
    windows = jnp.concatenate(
        [full[:, block * LANE : block * LANE + 2 * LANE] for block in range(blocks)], axis=0
    )
    filtered = jnp.dot(windows, band_ref[...], preferred_element_type=jnp.float32)
    filtered = filtered.astype(jnp.bfloat16)
    stacked = jnp.concatenate(
        [
            jnp.concatenate(
                [
                    filtered[block * rows : (block + 1) * rows, base * LANE : (base + 1) * LANE]
                    for block in range(blocks)
                ],
                axis=1,
            )
            for base in range(bases)
        ],
        axis=0,
    )
    out_ref[...] = acc_ref[...] + jnp.dot(mix_ref[...], stacked, preferred_element_type=jnp.float32)


def filter_mix(slab_image, tap_values, mix_matrix, acc):
    rows, width = slab_image.shape
    bases, taps = tap_values.shape
    padded = jnp.pad(slab_image, ((0, 0), (32, SPAN - 32)))
    band_rows = jnp.pad(tap_values, ((0, 0), (15, 2 * LANE + 1 - 15 - taps)))
    band = toeplitz(band_rows, LANE).transpose(2, 0, 1).reshape(2 * LANE, bases * LANE)
    steps = width // SPAN
    return pl.pallas_call(
        filter_mix_kernel,
        grid=(steps,),
        in_specs=[
            pl.BlockSpec((rows, SPAN), lambda k: (0, k)),
            pl.BlockSpec((rows, LANE), lambda k: (0, (k + 1) * (SPAN // LANE))),
            pl.BlockSpec((2 * LANE, bases * LANE), lambda k: (0, 0)),
            pl.BlockSpec((rows, bases * rows), lambda k: (0, 0)),
            pl.BlockSpec((rows, SPAN), lambda k: (0, k)),
        ],
        out_specs=pl.BlockSpec((rows, SPAN), lambda k: (0, k)),
        out_shape=jax.ShapeDtypeStruct((rows, width), jnp.float32),
        input_output_aliases={4: 0},
        cost_estimate=pl.CostEstimate(
            flops=2 * rows * width * 2 * LANE * bases + 2 * rows * width * bases * rows,
            transcendentals=0,
            bytes_accessed=padded.size * 2 + band.size * 2 + mix_matrix.size * 2 + acc.size * 8,
        ),
    )(padded, padded, band, mix_matrix, acc)


def visit_term(received, recv_off, shifts, weight, psf_index, coef_table, basis_x, basis_y, acc):
    warp_x = lanczos_taps(shifts[0])
    warp_y = lanczos_taps(shifts[1])
    slab_image = place(received, recv_off, warp_y).astype(jnp.bfloat16)
    tap_values = combined_taps(basis_x, warp_x).astype(jnp.bfloat16)
    class_hits = (psf_index == jnp.arange(coef_table.shape[0], dtype=jnp.int32)).astype(jnp.float32)
    coeffs = jnp.sum(class_hits[:, None] * coef_table, axis=0)
    mix_matrix = mixing(weight, coeffs, basis_y, SLAB_ROWS)
    return filter_mix(slab_image, tap_values, mix_matrix, acc)


def across_pairs(halves, rows):
    return [(h * rows + r, (halves - 1 - h) * rows + r) for h in range(halves) for r in range(rows)]


def shards(
    exposures, owners, offsets, visit_shift, visit_weight, psf_class, coef_table, basis_x, basis_y
):
    places = lax.axis_size(("x", "y"))
    halves = lax.axis_size("zh")
    rows_z = lax.axis_size("zl")
    streams = rows_z * lax.axis_size("c")
    half = lax.axis_index("zh")
    step_count = exposures.shape[0]
    width = exposures.shape[4]
    strip_rows = exposures.shape[3]
    fanout = owners.shape[3]
    strip_count = exposures.shape[2]
    table = jnp.concatenate([owners[:, 0], offsets[:, 0]], axis=2).reshape(-1)
    table_strip = jnp.zeros((1, strip_rows, width), exposures.dtype)
    table_strip = table_strip.at[0, 0, : table.shape[0]].set(table.astype(exposures.dtype))
    far_strips = []
    landed = None
    for step_index in range(step_count):
        strips = exposures[step_index, 0]
        if step_index == 0:
            strips = jnp.concatenate([strips, table_strip], axis=0)
        else:
            strips, _ = lax.optimization_barrier((strips, landed))
        landed = lax.ppermute(strips, ("zh", "zl"), across_pairs(halves, rows_z))
        far_strips.append(landed)
    far_table = far_strips[0][strip_count, 0, : table.shape[0]].astype(jnp.int32)
    far_table = far_table.reshape(step_count, strip_count, 2 * fanout)
    own = [
        pack(exposures[step_index, 0], owners[step_index, 0], offsets[step_index, 0], half, places)
        for step_index in range(step_count)
    ]
    far = [
        pack(
            far_strips[step_index][:strip_count],
            far_table[step_index, :, :fanout],
            far_table[step_index, :, fanout:],
            half,
            places,
        )
        for step_index in range(step_count)
    ]
    slot_offsets = jnp.stack(
        [jnp.concatenate([own[t][1], far[t][1]], axis=1) for t in range(step_count)], axis=1
    )
    recv_offsets = lax.all_to_all(slot_offsets, ("x", "y"), split_axis=0, concat_axis=0, tiled=True)
    outgoing = [
        jnp.concatenate([own[step_index][0], far[step_index][0]], axis=1)
        for step_index in range(step_count)
    ]
    received = [None] * step_count
    for step_index in range(min(2, step_count)):
        received[step_index] = lax.all_to_all(
            outgoing[step_index], ("x", "y"), split_axis=0, concat_axis=0, tiled=True
        )
    partial_sum = jnp.zeros((SLAB_ROWS, width), jnp.float32)
    for step_index in range(step_count):
        partial_sum = visit_term(
            received[step_index],
            recv_offsets[:, step_index],
            visit_shift[step_index, 0],
            visit_weight[step_index, 0],
            psf_class[step_index, 0],
            coef_table,
            basis_x,
            basis_y,
            partial_sum,
        )
        later = step_index + 2
        if later < step_count:
            released, partial_sum = lax.optimization_barrier((outgoing[later], partial_sum))
            received[later] = lax.all_to_all(
                released, ("x", "y"), split_axis=0, concat_axis=0, tiled=True
            )
    share_rows = SLAB_ROWS // streams
    pieces = lax.all_to_all(
        partial_sum.astype(jnp.bfloat16).reshape(streams, share_rows, width), ("zl", "c"),
        split_axis=0, concat_axis=0, tiled=True,
    )
    return jnp.sum(pieces.astype(jnp.float32), axis=0)


def solution(mesh):
    names = ("x", "y", "zh", "zl", "c")
    patches, streams = mesh.devices.shape
    fine = Mesh(mesh.devices.reshape(4, 4, patches // 16, streams // 2, 2), names)
    patch = ("x", "y", "zh")
    stream = ("zl", "c")
    placed = (
        P(None, stream, patch, None, None),
        P(None, stream, patch, None),
        P(None, stream, patch, None),
        P(None, stream, None),
        P(None, stream),
        P(None, stream),
        P(),
        P(),
        P(),
    )
    return jax.shard_map(
        shards, mesh=fine, in_specs=placed, out_specs=P(patch + stream, None), check_vma=False
    )
```

```python
import jax
import jax.numpy as jnp
from jax import lax
from jax.sharding import Mesh, PartitionSpec as P
from jax.experimental import pallas as pl

CAP = 2
SLAB_ROWS = 64


def lanczos_taps(fraction):
    distance = jnp.arange(6, dtype=jnp.int32).astype(jnp.float32) - 2.0 - fraction
    values = jnp.sinc(distance) * jnp.sinc(distance / 3.0)
    return values / jnp.sum(values)


def combined_taps(basis_rows, warp_x):
    summed = jnp.zeros((basis_rows.shape[0], basis_rows.shape[1] + 5), jnp.float32)
    for tap_slot in range(6):
        summed = summed + jnp.pad(basis_rows * warp_x[tap_slot], ((0, 0), (tap_slot, 5 - tap_slot)))
    return summed


def toeplitz(period, count):
    length = period.shape[-1] - 1
    tiled = jnp.tile(period, [1] * (period.ndim - 1) + [count])
    return tiled[..., : count * length].reshape(period.shape[:-1] + (count, length))


def row_filter(slab_image, tap_values):
    row_count = slab_image.shape[0]
    width = slab_image.shape[1]
    blocks = width // 128
    padded = jnp.pad(slab_image, ((0, 0), (32, 96)))
    front_part = padded[:, :width].reshape(row_count, blocks, 128)
    second = padded[:, 128 : width + 128].reshape(row_count, blocks, 128)[:, :, :64]
    windows = jnp.concatenate([front_part, second], axis=2)
    taps = tap_values.shape[1]
    band_rows = jnp.pad(tap_values, ((0, 0), (15, 193 - 15 - taps)))
    band_matrix = toeplitz(band_rows, 128)
    filtered = jnp.einsum("rna,boa->brno", windows, band_matrix, preferred_element_type=jnp.float32)
    return filtered.astype(jnp.bfloat16).reshape(tap_values.shape[0] * row_count, width)


def mixing(weight, coeffs, basis_y, row_count):
    reach = basis_y.shape[1] // 2
    period = jnp.pad(basis_y, ((0, 0), (0, row_count + reach + 1 - basis_y.shape[1])))
    kernel_table = toeplitz(period, row_count)[:, :, reach:]
    kernel_table = kernel_table * (weight * coeffs)[:, None, None]
    return kernel_table.astype(jnp.bfloat16).transpose(1, 0, 2).reshape(row_count, -1)


def pack(strips, owner_table, offset_table, half, places):
    strip_count = strips.shape[0]
    fanout = owner_table.shape[1]
    owner = owner_table.reshape(-1)
    target = jnp.where(owner % 2 == half, owner // 2, places)
    slots = places + 1
    target_hits = (target[:, None] == jnp.arange(slots, dtype=jnp.int32)[None, :]).astype(jnp.int32)
    earlier = jnp.cumsum(target_hits, axis=0) - target_hits
    position = jnp.sum(earlier * target_hits, axis=1)
    slot_index = target * CAP + position
    matches = (slot_index[None, :] == jnp.arange(places * CAP, dtype=jnp.int32)[:, None]).astype(
        jnp.int32
    )
    strip_select = jnp.sum(matches.reshape(places * CAP, strip_count, fanout), axis=2).astype(
        jnp.bfloat16
    )
    outgoing = jnp.dot(
        strip_select, strips.reshape(strip_count, -1), preferred_element_type=jnp.bfloat16
    )
    filled = jnp.sum(matches, axis=1)
    slot_offset = jnp.sum(matches * offset_table.reshape(-1)[None, :], axis=1) + (filled - 1) * (
        SLAB_ROWS + 8
    )
    return (
        outgoing.reshape(places, CAP, strips.shape[1], strips.shape[2]),
        slot_offset.reshape(places, CAP),
    )


def place(received, recv_off, warp_y):
    strip_rows = received.shape[-2]
    width = received.shape[-1]
    starts = recv_off.reshape(-1)
    local_row = jnp.arange(SLAB_ROWS, dtype=jnp.int32)[:, None] - starts[None, :]
    inside = (local_row >= 0) & (local_row < strip_rows)
    tap_index = jnp.arange(strip_rows, dtype=jnp.int32)[None, None, :] - local_row[:, :, None] + 2
    tap_hits = (tap_index[:, :, :, None] == jnp.arange(6, dtype=jnp.int32)).astype(jnp.float32)
    tap_values = jnp.sum(tap_hits * warp_y, axis=3)
    tap_values = (
        jnp.where(inside[:, :, None], tap_values, 0.0).astype(jnp.bfloat16).reshape(SLAB_ROWS, -1)
    )
    return jnp.dot(tap_values, received.reshape(-1, width), preferred_element_type=jnp.float32)


LANE = 128
SPAN = 512


def filter_mix_kernel(slab_ref, halo_ref, band_ref, mix_ref, acc_ref, out_ref):
    full = jnp.concatenate([slab_ref[...], halo_ref[...]], axis=1)
    rows = slab_ref.shape[0]
    blocks = SPAN // LANE
    bases = band_ref.shape[1] // LANE
    windows = jnp.concatenate(
        [full[:, block * LANE : block * LANE + 2 * LANE] for block in range(blocks)], axis=0
    )
    filtered = jnp.dot(windows, band_ref[...], preferred_element_type=jnp.float32)
    filtered = filtered.astype(jnp.bfloat16)
    stacked = jnp.concatenate(
        [
            jnp.concatenate(
                [
                    filtered[block * rows : (block + 1) * rows, base * LANE : (base + 1) * LANE]
                    for block in range(blocks)
                ],
                axis=1,
            )
            for base in range(bases)
        ],
        axis=0,
    )
    out_ref[...] = acc_ref[...] + jnp.dot(mix_ref[...], stacked, preferred_element_type=jnp.float32)


def filter_mix(slab_image, tap_values, mix_matrix, acc):
    rows, width = slab_image.shape
    bases, taps = tap_values.shape
    padded = jnp.pad(slab_image, ((0, 0), (32, SPAN - 32)))
    band_rows = jnp.pad(tap_values, ((0, 0), (15, 2 * LANE + 1 - 15 - taps)))
    band = toeplitz(band_rows, LANE).transpose(2, 0, 1).reshape(2 * LANE, bases * LANE)
    steps = width // SPAN
    return pl.pallas_call(
        filter_mix_kernel,
        grid=(steps,),
        in_specs=[
            pl.BlockSpec((rows, SPAN), lambda k: (0, k)),
            pl.BlockSpec((rows, LANE), lambda k: (0, (k + 1) * (SPAN // LANE))),
            pl.BlockSpec((2 * LANE, bases * LANE), lambda k: (0, 0)),
            pl.BlockSpec((rows, bases * rows), lambda k: (0, 0)),
            pl.BlockSpec((rows, SPAN), lambda k: (0, k)),
        ],
        out_specs=pl.BlockSpec((rows, SPAN), lambda k: (0, k)),
        out_shape=jax.ShapeDtypeStruct((rows, width), jnp.float32),
        input_output_aliases={4: 0},
        cost_estimate=pl.CostEstimate(
            flops=2 * rows * width * 2 * LANE * bases + 2 * rows * width * bases * rows,
            transcendentals=0,
            bytes_accessed=padded.size * 2 + band.size * 2 + mix_matrix.size * 2 + acc.size * 8,
        ),
    )(padded, padded, band, mix_matrix, acc)


def visit_term(received, recv_off, shifts, weight, psf_index, coef_table, basis_x, basis_y, acc):
    warp_x = lanczos_taps(shifts[0])
    warp_y = lanczos_taps(shifts[1])
    slab_image = place(received, recv_off, warp_y).astype(jnp.bfloat16)
    tap_values = combined_taps(basis_x, warp_x).astype(jnp.bfloat16)
    class_hits = (psf_index == jnp.arange(coef_table.shape[0], dtype=jnp.int32)).astype(jnp.float32)
    coeffs = jnp.sum(class_hits[:, None] * coef_table, axis=0)
    mix_matrix = mixing(weight, coeffs, basis_y, SLAB_ROWS)
    return filter_mix(slab_image, tap_values, mix_matrix, acc)


def across_pairs(halves, rows):
    return [(h * rows + r, (halves - 1 - h) * rows + r) for h in range(halves) for r in range(rows)]


def shards(
    exposures, owners, offsets, visit_shift, visit_weight, psf_class, coef_table, basis_x, basis_y
):
    places = lax.axis_size(("x", "y"))
    halves = lax.axis_size("zh")
    rows_z = lax.axis_size("zl")
    streams = rows_z * lax.axis_size("c")
    half = lax.axis_index("zh")
    step_count = exposures.shape[0]
    width = exposures.shape[4]
    strip_rows = exposures.shape[3]
    fanout = owners.shape[3]
    strip_count = exposures.shape[2]
    table = jnp.concatenate([owners[:, 0], offsets[:, 0]], axis=2).reshape(-1)
    table_strip = jnp.zeros((1, strip_rows, width), exposures.dtype)
    table_strip = table_strip.at[0, 0, : table.shape[0]].set(table.astype(exposures.dtype))
    far_strips = []
    landed = None
    for step_index in range(step_count):
        strips = exposures[step_index, 0]
        if step_index == 0:
            strips = jnp.concatenate([strips, table_strip], axis=0)
        elif step_index > 1:
            strips, _ = lax.optimization_barrier((strips, landed))
        landed = lax.ppermute(strips, ("zh", "zl"), across_pairs(halves, rows_z))
        far_strips.append(landed)
    far_table = far_strips[0][strip_count, 0, : table.shape[0]].astype(jnp.int32)
    far_table = far_table.reshape(step_count, strip_count, 2 * fanout)
    own = [
        pack(exposures[step_index, 0], owners[step_index, 0], offsets[step_index, 0], half, places)
        for step_index in range(step_count)
    ]
    far = [
        pack(
            far_strips[step_index][:strip_count],
            far_table[step_index, :, :fanout],
            far_table[step_index, :, fanout:],
            half,
            places,
        )
        for step_index in range(step_count)
    ]
    slot_offsets = jnp.stack(
        [jnp.concatenate([own[t][1], far[t][1]], axis=1) for t in range(step_count)], axis=1
    )
    recv_offsets = lax.all_to_all(slot_offsets, ("x", "y"), split_axis=0, concat_axis=0, tiled=True)
    outgoing = [
        jnp.concatenate([own[step_index][0], far[step_index][0]], axis=1)
        for step_index in range(step_count)
    ]
    received = [None] * step_count
    for step_index in range(min(2, step_count)):
        received[step_index] = lax.all_to_all(
            outgoing[step_index], ("x", "y"), split_axis=0, concat_axis=0, tiled=True
        )
    partial_sum = jnp.zeros((SLAB_ROWS, width), jnp.float32)
    for step_index in range(step_count):
        partial_sum = visit_term(
            received[step_index],
            recv_offsets[:, step_index],
            visit_shift[step_index, 0],
            visit_weight[step_index, 0],
            psf_class[step_index, 0],
            coef_table,
            basis_x,
            basis_y,
            partial_sum,
        )
        later = step_index + 2
        if later < step_count:
            released, partial_sum = lax.optimization_barrier((outgoing[later], partial_sum))
            received[later] = lax.all_to_all(
                released, ("x", "y"), split_axis=0, concat_axis=0, tiled=True
            )
    share_rows = SLAB_ROWS // streams
    pieces = lax.all_to_all(
        partial_sum.astype(jnp.bfloat16).reshape(streams, share_rows, width), ("zl", "c"),
        split_axis=0, concat_axis=0, tiled=True,
    )
    return jnp.sum(pieces.astype(jnp.float32), axis=0)


def solution(mesh):
    names = ("x", "y", "zh", "zl", "c")
    patches, streams = mesh.devices.shape
    fine = Mesh(mesh.devices.reshape(4, 4, patches // 16, streams // 2, 2), names)
    patch = ("x", "y", "zh")
    stream = ("zl", "c")
    placed = (
        P(None, stream, patch, None, None),
        P(None, stream, patch, None),
        P(None, stream, patch, None),
        P(None, stream, None),
        P(None, stream),
        P(None, stream),
        P(),
        P(),
        P(),
    )
    return jax.shard_map(
        shards, mesh=fine, in_specs=placed, out_specs=P(patch + stream, None), check_vma=False
    )
```

```python
import jax
import jax.numpy as jnp
from jax import lax
from jax.sharding import Mesh, PartitionSpec as P
from jax.experimental import pallas as pl

CAP = 2
SLAB_ROWS = 64


def lanczos_taps(fraction):
    distance = jnp.arange(6, dtype=jnp.int32).astype(jnp.float32) - 2.0 - fraction
    values = jnp.sinc(distance) * jnp.sinc(distance / 3.0)
    return values / jnp.sum(values)


def combined_taps(basis_rows, warp_x):
    summed = jnp.zeros((basis_rows.shape[0], basis_rows.shape[1] + 5), jnp.float32)
    for tap_slot in range(6):
        summed = summed + jnp.pad(basis_rows * warp_x[tap_slot], ((0, 0), (tap_slot, 5 - tap_slot)))
    return summed


def toeplitz(period, count):
    length = period.shape[-1] - 1
    tiled = jnp.tile(period, [1] * (period.ndim - 1) + [count])
    return tiled[..., : count * length].reshape(period.shape[:-1] + (count, length))


def row_filter(slab_image, tap_values):
    row_count = slab_image.shape[0]
    width = slab_image.shape[1]
    blocks = width // 128
    padded = jnp.pad(slab_image, ((0, 0), (32, 96)))
    front_part = padded[:, :width].reshape(row_count, blocks, 128)
    second = padded[:, 128 : width + 128].reshape(row_count, blocks, 128)[:, :, :64]
    windows = jnp.concatenate([front_part, second], axis=2)
    taps = tap_values.shape[1]
    band_rows = jnp.pad(tap_values, ((0, 0), (15, 193 - 15 - taps)))
    band_matrix = toeplitz(band_rows, 128)
    filtered = jnp.einsum("rna,boa->brno", windows, band_matrix, preferred_element_type=jnp.float32)
    return filtered.astype(jnp.bfloat16).reshape(tap_values.shape[0] * row_count, width)


def mixing(weight, coeffs, basis_y, row_count):
    reach = basis_y.shape[1] // 2
    period = jnp.pad(basis_y, ((0, 0), (0, row_count + reach + 1 - basis_y.shape[1])))
    kernel_table = toeplitz(period, row_count)[:, :, reach:]
    kernel_table = kernel_table * (weight * coeffs)[:, None, None]
    return kernel_table.astype(jnp.bfloat16).transpose(1, 0, 2).reshape(row_count, -1)


def pack(strips, owner_table, offset_table, half, places):
    strip_count = strips.shape[0]
    fanout = owner_table.shape[1]
    owner = owner_table.reshape(-1)
    target = jnp.where(owner % 2 == half, owner // 2, places)
    slots = places + 1
    target_hits = (target[:, None] == jnp.arange(slots, dtype=jnp.int32)[None, :]).astype(jnp.int32)
    earlier = jnp.cumsum(target_hits, axis=0) - target_hits
    position = jnp.sum(earlier * target_hits, axis=1)
    slot_index = target * CAP + position
    matches = (slot_index[None, :] == jnp.arange(places * CAP, dtype=jnp.int32)[:, None]).astype(
        jnp.int32
    )
    strip_select = jnp.sum(matches.reshape(places * CAP, strip_count, fanout), axis=2).astype(
        jnp.bfloat16
    )
    outgoing = jnp.dot(
        strip_select, strips.reshape(strip_count, -1), preferred_element_type=jnp.bfloat16
    )
    filled = jnp.sum(matches, axis=1)
    slot_offset = jnp.sum(matches * offset_table.reshape(-1)[None, :], axis=1) + (filled - 1) * (
        SLAB_ROWS + 8
    )
    return (
        outgoing.reshape(places, CAP, strips.shape[1], strips.shape[2]),
        slot_offset.reshape(places, CAP),
    )


def place(received, recv_off, warp_y):
    strip_rows = received.shape[-2]
    width = received.shape[-1]
    starts = recv_off.reshape(-1)
    local_row = jnp.arange(SLAB_ROWS, dtype=jnp.int32)[:, None] - starts[None, :]
    inside = (local_row >= 0) & (local_row < strip_rows)
    tap_index = jnp.arange(strip_rows, dtype=jnp.int32)[None, None, :] - local_row[:, :, None] + 2
    tap_hits = (tap_index[:, :, :, None] == jnp.arange(6, dtype=jnp.int32)).astype(jnp.float32)
    tap_values = jnp.sum(tap_hits * warp_y, axis=3)
    tap_values = (
        jnp.where(inside[:, :, None], tap_values, 0.0).astype(jnp.bfloat16).reshape(SLAB_ROWS, -1)
    )
    return jnp.dot(tap_values, received.reshape(-1, width), preferred_element_type=jnp.float32)


LANE = 128
SPAN = 512


def filter_mix_kernel(slab_ref, halo_ref, band_ref, mix_ref, acc_ref, out_ref):
    full = jnp.concatenate([slab_ref[...], halo_ref[...]], axis=1)
    rows = slab_ref.shape[0]
    blocks = SPAN // LANE
    bases = band_ref.shape[1] // LANE
    windows = jnp.concatenate(
        [full[:, block * LANE : block * LANE + 2 * LANE] for block in range(blocks)], axis=0
    )
    filtered = jnp.dot(windows, band_ref[...], preferred_element_type=jnp.float32)
    filtered = filtered.astype(jnp.bfloat16)
    stacked = jnp.concatenate(
        [
            jnp.concatenate(
                [
                    filtered[block * rows : (block + 1) * rows, base * LANE : (base + 1) * LANE]
                    for block in range(blocks)
                ],
                axis=1,
            )
            for base in range(bases)
        ],
        axis=0,
    )
    out_ref[...] = acc_ref[...] + jnp.dot(mix_ref[...], stacked, preferred_element_type=jnp.float32)


def filter_mix(slab_image, tap_values, mix_matrix, acc):
    rows, width = slab_image.shape
    bases, taps = tap_values.shape
    padded = jnp.pad(slab_image, ((0, 0), (32, SPAN - 32)))
    band_rows = jnp.pad(tap_values, ((0, 0), (15, 2 * LANE + 1 - 15 - taps)))
    band = toeplitz(band_rows, LANE).transpose(2, 0, 1).reshape(2 * LANE, bases * LANE)
    steps = width // SPAN
    return pl.pallas_call(
        filter_mix_kernel,
        grid=(steps,),
        in_specs=[
            pl.BlockSpec((rows, SPAN), lambda k: (0, k)),
            pl.BlockSpec((rows, LANE), lambda k: (0, (k + 1) * (SPAN // LANE))),
            pl.BlockSpec((2 * LANE, bases * LANE), lambda k: (0, 0)),
            pl.BlockSpec((rows, bases * rows), lambda k: (0, 0)),
            pl.BlockSpec((rows, SPAN), lambda k: (0, k)),
        ],
        out_specs=pl.BlockSpec((rows, SPAN), lambda k: (0, k)),
        out_shape=jax.ShapeDtypeStruct((rows, width), jnp.float32),
        input_output_aliases={4: 0},
        cost_estimate=pl.CostEstimate(
            flops=2 * rows * width * 2 * LANE * bases + 2 * rows * width * bases * rows,
            transcendentals=0,
            bytes_accessed=padded.size * 2 + band.size * 2 + mix_matrix.size * 2 + acc.size * 8,
        ),
    )(padded, padded, band, mix_matrix, acc)


def visit_term(received, recv_off, shifts, weight, psf_index, coef_table, basis_x, basis_y, acc):
    warp_x = lanczos_taps(shifts[0])
    warp_y = lanczos_taps(shifts[1])
    slab_image = place(received, recv_off, warp_y).astype(jnp.bfloat16)
    tap_values = combined_taps(basis_x, warp_x).astype(jnp.bfloat16)
    class_hits = (psf_index == jnp.arange(coef_table.shape[0], dtype=jnp.int32)).astype(jnp.float32)
    coeffs = jnp.sum(class_hits[:, None] * coef_table, axis=0)
    mix_matrix = mixing(weight, coeffs, basis_y, SLAB_ROWS)
    return filter_mix(slab_image, tap_values, mix_matrix, acc)


def across_pairs(halves, rows):
    return [(h * rows + r, (halves - 1 - h) * rows + r) for h in range(halves) for r in range(rows)]


def shards(
    exposures, owners, offsets, visit_shift, visit_weight, psf_class, coef_table, basis_x, basis_y
):
    places = lax.axis_size(("x", "y"))
    halves = lax.axis_size("zh")
    rows_z = lax.axis_size("zl")
    streams = rows_z * lax.axis_size("c")
    half = lax.axis_index("zh")
    step_count = exposures.shape[0]
    width = exposures.shape[4]
    strip_rows = exposures.shape[3]
    fanout = owners.shape[3]
    strip_count = exposures.shape[2]
    table = jnp.concatenate([owners[:, 0], offsets[:, 0]], axis=2).reshape(-1)
    table_strip = jnp.zeros((1, strip_rows, width), exposures.dtype)
    table_strip = table_strip.at[0, 0, : table.shape[0]].set(table.astype(exposures.dtype))
    far_strips = []
    for step_index in range(step_count):
        strips = exposures[step_index, 0]
        if step_index == 0:
            strips = jnp.concatenate([strips, table_strip], axis=0)
        elif step_index > 1:
            strips, _ = lax.optimization_barrier((strips, far_strips[step_index - 2]))
        far_strips.append(lax.ppermute(strips, ("zh", "zl"), across_pairs(halves, rows_z)))
    far_table = far_strips[0][strip_count, 0, : table.shape[0]].astype(jnp.int32)
    far_table = far_table.reshape(step_count, strip_count, 2 * fanout)
    own = [
        pack(exposures[step_index, 0], owners[step_index, 0], offsets[step_index, 0], half, places)
        for step_index in range(step_count)
    ]
    far = [
        pack(
            far_strips[step_index][:strip_count],
            far_table[step_index, :, :fanout],
            far_table[step_index, :, fanout:],
            half,
            places,
        )
        for step_index in range(step_count)
    ]
    slot_offsets = jnp.stack(
        [jnp.concatenate([own[t][1], far[t][1]], axis=1) for t in range(step_count)], axis=1
    )
    recv_offsets = lax.all_to_all(slot_offsets, ("x", "y"), split_axis=0, concat_axis=0, tiled=True)
    outgoing = [
        jnp.concatenate([own[step_index][0], far[step_index][0]], axis=1)
        for step_index in range(step_count)
    ]
    received = [None] * step_count
    for step_index in range(min(2, step_count)):
        released = outgoing[step_index]
        if 0 < step_index < step_count - 1:
            released, _ = lax.optimization_barrier((released, far_strips[step_index + 1]))
        received[step_index] = lax.all_to_all(
            released, ("x", "y"), split_axis=0, concat_axis=0, tiled=True
        )
    partial_sum = jnp.zeros((SLAB_ROWS, width), jnp.float32)
    for step_index in range(step_count):
        partial_sum = visit_term(
            received[step_index],
            recv_offsets[:, step_index],
            visit_shift[step_index, 0],
            visit_weight[step_index, 0],
            psf_class[step_index, 0],
            coef_table,
            basis_x,
            basis_y,
            partial_sum,
        )
        later = step_index + 2
        if later < step_count:
            released, partial_sum = lax.optimization_barrier((outgoing[later], partial_sum))
            if later < step_count - 1:
                released, _ = lax.optimization_barrier((released, far_strips[later + 1]))
            received[later] = lax.all_to_all(
                released, ("x", "y"), split_axis=0, concat_axis=0, tiled=True
            )
    share_rows = SLAB_ROWS // streams
    pieces = lax.all_to_all(
        partial_sum.astype(jnp.bfloat16).reshape(streams, share_rows, width), ("zl", "c"),
        split_axis=0, concat_axis=0, tiled=True,
    )
    return jnp.sum(pieces.astype(jnp.float32), axis=0)


def solution(mesh):
    names = ("x", "y", "zh", "zl", "c")
    patches, streams = mesh.devices.shape
    fine = Mesh(mesh.devices.reshape(4, 4, patches // 16, streams // 2, 2), names)
    patch = ("x", "y", "zh")
    stream = ("zl", "c")
    placed = (
        P(None, stream, patch, None, None),
        P(None, stream, patch, None),
        P(None, stream, patch, None),
        P(None, stream, None),
        P(None, stream),
        P(None, stream),
        P(),
        P(),
        P(),
    )
    return jax.shard_map(
        shards, mesh=fine, in_specs=placed, out_specs=P(patch + stream, None), check_vma=False
    )
```

```python
import jax
import jax.numpy as jnp
from jax import lax
from jax.sharding import Mesh, PartitionSpec as P
from jax.experimental import pallas as pl

CAP = 2
SLAB_ROWS = 64


def lanczos_taps(fraction):
    distance = jnp.arange(6, dtype=jnp.int32).astype(jnp.float32) - 2.0 - fraction
    values = jnp.sinc(distance) * jnp.sinc(distance / 3.0)
    return values / jnp.sum(values)


def combined_taps(basis_rows, warp_x):
    summed = jnp.zeros((basis_rows.shape[0], basis_rows.shape[1] + 5), jnp.float32)
    for tap_slot in range(6):
        summed = summed + jnp.pad(basis_rows * warp_x[tap_slot], ((0, 0), (tap_slot, 5 - tap_slot)))
    return summed


def toeplitz(period, count):
    length = period.shape[-1] - 1
    tiled = jnp.tile(period, [1] * (period.ndim - 1) + [count])
    return tiled[..., : count * length].reshape(period.shape[:-1] + (count, length))


def row_filter(slab_image, tap_values):
    row_count = slab_image.shape[0]
    width = slab_image.shape[1]
    blocks = width // 128
    padded = jnp.pad(slab_image, ((0, 0), (32, 96)))
    front_part = padded[:, :width].reshape(row_count, blocks, 128)
    second = padded[:, 128 : width + 128].reshape(row_count, blocks, 128)[:, :, :64]
    windows = jnp.concatenate([front_part, second], axis=2)
    taps = tap_values.shape[1]
    band_rows = jnp.pad(tap_values, ((0, 0), (15, 193 - 15 - taps)))
    band_matrix = toeplitz(band_rows, 128)
    filtered = jnp.einsum("rna,boa->brno", windows, band_matrix, preferred_element_type=jnp.float32)
    return filtered.astype(jnp.bfloat16).reshape(tap_values.shape[0] * row_count, width)


def mixing(weight, coeffs, basis_y, row_count):
    reach = basis_y.shape[1] // 2
    period = jnp.pad(basis_y, ((0, 0), (0, row_count + reach + 1 - basis_y.shape[1])))
    kernel_table = toeplitz(period, row_count)[:, :, reach:]
    kernel_table = kernel_table * (weight * coeffs)[:, None, None]
    return kernel_table.astype(jnp.bfloat16).transpose(1, 0, 2).reshape(row_count, -1)


def pack(strips, owner_table, offset_table, half, places):
    strip_count = strips.shape[0]
    fanout = owner_table.shape[1]
    owner = owner_table.reshape(-1)
    target = jnp.where(owner % 2 == half, owner // 2, places)
    slots = places + 1
    target_hits = (target[:, None] == jnp.arange(slots, dtype=jnp.int32)[None, :]).astype(jnp.int32)
    earlier = jnp.cumsum(target_hits, axis=0) - target_hits
    position = jnp.sum(earlier * target_hits, axis=1)
    slot_index = target * CAP + position
    matches = (slot_index[None, :] == jnp.arange(places * CAP, dtype=jnp.int32)[:, None]).astype(
        jnp.int32
    )
    strip_select = jnp.sum(matches.reshape(places * CAP, strip_count, fanout), axis=2).astype(
        jnp.bfloat16
    )
    outgoing = jnp.dot(
        strip_select, strips.reshape(strip_count, -1), preferred_element_type=jnp.bfloat16
    )
    filled = jnp.sum(matches, axis=1)
    slot_offset = jnp.sum(matches * offset_table.reshape(-1)[None, :], axis=1) + (filled - 1) * (
        SLAB_ROWS + 8
    )
    return (
        outgoing.reshape(places, CAP, strips.shape[1], strips.shape[2]),
        slot_offset.reshape(places, CAP),
    )


def place(received, recv_off, warp_y):
    strip_rows = received.shape[-2]
    width = received.shape[-1]
    starts = recv_off.reshape(-1)
    local_row = jnp.arange(SLAB_ROWS, dtype=jnp.int32)[:, None] - starts[None, :]
    inside = (local_row >= 0) & (local_row < strip_rows)
    tap_index = jnp.arange(strip_rows, dtype=jnp.int32)[None, None, :] - local_row[:, :, None] + 2
    tap_hits = (tap_index[:, :, :, None] == jnp.arange(6, dtype=jnp.int32)).astype(jnp.float32)
    tap_values = jnp.sum(tap_hits * warp_y, axis=3)
    tap_values = (
        jnp.where(inside[:, :, None], tap_values, 0.0).astype(jnp.bfloat16).reshape(SLAB_ROWS, -1)
    )
    return jnp.dot(tap_values, received.reshape(-1, width), preferred_element_type=jnp.float32)


LANE = 128
SPAN = 1024


def filter_mix_kernel(slab_ref, halo_ref, band_ref, mix_ref, acc_ref, out_ref):
    full = jnp.concatenate([slab_ref[...], halo_ref[...]], axis=1)
    rows = slab_ref.shape[0]
    blocks = SPAN // LANE
    bases = band_ref.shape[1] // LANE
    windows = jnp.concatenate(
        [full[:, block * LANE : block * LANE + 2 * LANE] for block in range(blocks)], axis=0
    )
    filtered = jnp.dot(windows, band_ref[...], preferred_element_type=jnp.float32)
    filtered = filtered.astype(jnp.bfloat16)
    stacked = jnp.concatenate(
        [
            jnp.concatenate(
                [
                    filtered[block * rows : (block + 1) * rows, base * LANE : (base + 1) * LANE]
                    for block in range(blocks)
                ],
                axis=1,
            )
            for base in range(bases)
        ],
        axis=0,
    )
    out_ref[...] = acc_ref[...] + jnp.dot(mix_ref[...], stacked, preferred_element_type=jnp.float32)


def filter_mix(slab_image, tap_values, mix_matrix, acc):
    rows, width = slab_image.shape
    bases, taps = tap_values.shape
    padded = jnp.pad(slab_image, ((0, 0), (32, SPAN - 32)))
    band_rows = jnp.pad(tap_values, ((0, 0), (15, 2 * LANE + 1 - 15 - taps)))
    band = toeplitz(band_rows, LANE).transpose(2, 0, 1).reshape(2 * LANE, bases * LANE)
    steps = width // SPAN
    return pl.pallas_call(
        filter_mix_kernel,
        grid=(steps,),
        in_specs=[
            pl.BlockSpec((rows, SPAN), lambda k: (0, k)),
            pl.BlockSpec((rows, LANE), lambda k: (0, (k + 1) * (SPAN // LANE))),
            pl.BlockSpec((2 * LANE, bases * LANE), lambda k: (0, 0)),
            pl.BlockSpec((rows, bases * rows), lambda k: (0, 0)),
            pl.BlockSpec((rows, SPAN), lambda k: (0, k)),
        ],
        out_specs=pl.BlockSpec((rows, SPAN), lambda k: (0, k)),
        out_shape=jax.ShapeDtypeStruct((rows, width), jnp.float32),
        input_output_aliases={4: 0},
        cost_estimate=pl.CostEstimate(
            flops=2 * rows * width * 2 * LANE * bases + 2 * rows * width * bases * rows,
            transcendentals=0,
            bytes_accessed=padded.size * 2 + band.size * 2 + mix_matrix.size * 2 + acc.size * 8,
        ),
    )(padded, padded, band, mix_matrix, acc)


def visit_term(received, recv_off, shifts, weight, psf_index, coef_table, basis_x, basis_y, acc):
    warp_x = lanczos_taps(shifts[0])
    warp_y = lanczos_taps(shifts[1])
    slab_image = place(received, recv_off, warp_y).astype(jnp.bfloat16)
    tap_values = combined_taps(basis_x, warp_x).astype(jnp.bfloat16)
    class_hits = (psf_index == jnp.arange(coef_table.shape[0], dtype=jnp.int32)).astype(jnp.float32)
    coeffs = jnp.sum(class_hits[:, None] * coef_table, axis=0)
    mix_matrix = mixing(weight, coeffs, basis_y, SLAB_ROWS)
    return filter_mix(slab_image, tap_values, mix_matrix, acc)


def across_pairs(halves, rows):
    return [(h * rows + r, (halves - 1 - h) * rows + r) for h in range(halves) for r in range(rows)]


def shards(
    exposures, owners, offsets, visit_shift, visit_weight, psf_class, coef_table, basis_x, basis_y
):
    places = lax.axis_size(("x", "y"))
    halves = lax.axis_size("zh")
    rows_z = lax.axis_size("zl")
    streams = rows_z * lax.axis_size("c")
    half = lax.axis_index("zh")
    step_count = exposures.shape[0]
    width = exposures.shape[4]
    strip_rows = exposures.shape[3]
    fanout = owners.shape[3]
    strip_count = exposures.shape[2]
    table = jnp.concatenate([owners[:, 0], offsets[:, 0]], axis=2).reshape(-1)
    table_strip = jnp.zeros((1, strip_rows, width), exposures.dtype)
    table_strip = table_strip.at[0, 0, : table.shape[0]].set(table.astype(exposures.dtype))
    far_strips = []
    for step_index in range(step_count):
        strips = exposures[step_index, 0]
        if step_index == 0:
            strips = jnp.concatenate([strips, table_strip], axis=0)
        elif step_index > 1:
            strips, _ = lax.optimization_barrier((strips, far_strips[step_index - 2]))
        far_strips.append(lax.ppermute(strips, ("zh", "zl"), across_pairs(halves, rows_z)))
    far_table = far_strips[0][strip_count, 0, : table.shape[0]].astype(jnp.int32)
    far_table = far_table.reshape(step_count, strip_count, 2 * fanout)
    own = [
        pack(exposures[step_index, 0], owners[step_index, 0], offsets[step_index, 0], half, places)
        for step_index in range(step_count)
    ]
    far = [
        pack(
            far_strips[step_index][:strip_count],
            far_table[step_index, :, :fanout],
            far_table[step_index, :, fanout:],
            half,
            places,
        )
        for step_index in range(step_count)
    ]
    slot_offsets = jnp.stack(
        [jnp.concatenate([own[t][1], far[t][1]], axis=1) for t in range(step_count)], axis=1
    )
    recv_offsets = lax.all_to_all(slot_offsets, ("x", "y"), split_axis=0, concat_axis=0, tiled=True)
    outgoing = [
        jnp.concatenate([own[step_index][0], far[step_index][0]], axis=1)
        for step_index in range(step_count)
    ]
    received = [None] * step_count
    for step_index in range(min(2, step_count)):
        released = outgoing[step_index]
        if 0 < step_index < step_count - 1:
            released, _ = lax.optimization_barrier((released, far_strips[step_index + 1]))
        received[step_index] = lax.all_to_all(
            released, ("x", "y"), split_axis=0, concat_axis=0, tiled=True
        )
    partial_sum = jnp.zeros((SLAB_ROWS, width), jnp.float32)
    for step_index in range(step_count):
        partial_sum = visit_term(
            received[step_index],
            recv_offsets[:, step_index],
            visit_shift[step_index, 0],
            visit_weight[step_index, 0],
            psf_class[step_index, 0],
            coef_table,
            basis_x,
            basis_y,
            partial_sum,
        )
        later = step_index + 2
        if later < step_count:
            released, partial_sum = lax.optimization_barrier((outgoing[later], partial_sum))
            if later < step_count - 1:
                released, _ = lax.optimization_barrier((released, far_strips[later + 1]))
            received[later] = lax.all_to_all(
                released, ("x", "y"), split_axis=0, concat_axis=0, tiled=True
            )
    share_rows = SLAB_ROWS // streams
    pieces = lax.all_to_all(
        partial_sum.astype(jnp.bfloat16).reshape(streams, share_rows, width), ("zl", "c"),
        split_axis=0, concat_axis=0, tiled=True,
    )
    return jnp.sum(pieces.astype(jnp.float32), axis=0)


def solution(mesh):
    names = ("x", "y", "zh", "zl", "c")
    patches, streams = mesh.devices.shape
    fine = Mesh(mesh.devices.reshape(4, 4, patches // 16, streams // 2, 2), names)
    patch = ("x", "y", "zh")
    stream = ("zl", "c")
    placed = (
        P(None, stream, patch, None, None),
        P(None, stream, patch, None),
        P(None, stream, patch, None),
        P(None, stream, None),
        P(None, stream),
        P(None, stream),
        P(),
        P(),
        P(),
    )
    return jax.shard_map(
        shards, mesh=fine, in_specs=placed, out_specs=P(patch + stream, None), check_vma=False
    )
```

```python
import jax
import jax.numpy as jnp
from jax import lax
from jax.sharding import Mesh, PartitionSpec as P
from jax.experimental import pallas as pl

CAP = 2
SLAB_ROWS = 64


def lanczos_taps(fraction):
    distance = jnp.arange(6, dtype=jnp.int32).astype(jnp.float32) - 2.0 - fraction
    values = jnp.sinc(distance) * jnp.sinc(distance / 3.0)
    return values / jnp.sum(values)


def combined_taps(basis_rows, warp_x):
    summed = jnp.zeros((basis_rows.shape[0], basis_rows.shape[1] + 5), jnp.float32)
    for tap_slot in range(6):
        summed = summed + jnp.pad(basis_rows * warp_x[tap_slot], ((0, 0), (tap_slot, 5 - tap_slot)))
    return summed


def toeplitz(period, count):
    length = period.shape[-1] - 1
    tiled = jnp.tile(period, [1] * (period.ndim - 1) + [count])
    return tiled[..., : count * length].reshape(period.shape[:-1] + (count, length))


def row_filter(slab_image, tap_values):
    row_count = slab_image.shape[0]
    width = slab_image.shape[1]
    blocks = width // 128
    padded = jnp.pad(slab_image, ((0, 0), (32, 96)))
    front_part = padded[:, :width].reshape(row_count, blocks, 128)
    second = padded[:, 128 : width + 128].reshape(row_count, blocks, 128)[:, :, :64]
    windows = jnp.concatenate([front_part, second], axis=2)
    taps = tap_values.shape[1]
    band_rows = jnp.pad(tap_values, ((0, 0), (15, 193 - 15 - taps)))
    band_matrix = toeplitz(band_rows, 128)
    filtered = jnp.einsum("rna,boa->brno", windows, band_matrix, preferred_element_type=jnp.float32)
    return filtered.astype(jnp.bfloat16).reshape(tap_values.shape[0] * row_count, width)


def mixing(weight, coeffs, basis_y, row_count):
    reach = basis_y.shape[1] // 2
    period = jnp.pad(basis_y, ((0, 0), (0, row_count + reach + 1 - basis_y.shape[1])))
    kernel_table = toeplitz(period, row_count)[:, :, reach:]
    kernel_table = kernel_table * (weight * coeffs)[:, None, None]
    return kernel_table.astype(jnp.bfloat16).transpose(1, 0, 2).reshape(row_count, -1)


def pack(strips, owner_table, offset_table, half, places):
    strip_count = strips.shape[0]
    fanout = owner_table.shape[1]
    owner = owner_table.reshape(-1)
    target = jnp.where(owner % 2 == half, owner // 2, places)
    slots = places + 1
    target_hits = (target[:, None] == jnp.arange(slots, dtype=jnp.int32)[None, :]).astype(jnp.int32)
    earlier = jnp.cumsum(target_hits, axis=0) - target_hits
    position = jnp.sum(earlier * target_hits, axis=1)
    slot_index = target * CAP + position
    matches = (slot_index[None, :] == jnp.arange(places * CAP, dtype=jnp.int32)[:, None]).astype(
        jnp.int32
    )
    strip_select = jnp.sum(matches.reshape(places * CAP, strip_count, fanout), axis=2).astype(
        jnp.bfloat16
    )
    outgoing = jnp.dot(
        strip_select, strips.reshape(strip_count, -1), preferred_element_type=jnp.bfloat16
    )
    filled = jnp.sum(matches, axis=1)
    slot_offset = jnp.sum(matches * offset_table.reshape(-1)[None, :], axis=1) + (filled - 1) * (
        SLAB_ROWS + 8
    )
    return (
        outgoing.reshape(places, CAP, strips.shape[1], strips.shape[2]),
        slot_offset.reshape(places, CAP),
    )


def place(received, recv_off, warp_y):
    strip_rows = received.shape[-2]
    width = received.shape[-1]
    starts = recv_off.reshape(-1)
    local_row = jnp.arange(SLAB_ROWS, dtype=jnp.int32)[:, None] - starts[None, :]
    inside = (local_row >= 0) & (local_row < strip_rows)
    tap_index = jnp.arange(strip_rows, dtype=jnp.int32)[None, None, :] - local_row[:, :, None] + 2
    tap_hits = (tap_index[:, :, :, None] == jnp.arange(6, dtype=jnp.int32)).astype(jnp.float32)
    tap_values = jnp.sum(tap_hits * warp_y, axis=3)
    tap_values = (
        jnp.where(inside[:, :, None], tap_values, 0.0).astype(jnp.bfloat16).reshape(SLAB_ROWS, -1)
    )
    return jnp.dot(tap_values, received.reshape(-1, width), preferred_element_type=jnp.float32)


LANE = 128
SPAN = 1024


def filter_mix_kernel(slab_ref, halo_ref, band_ref, mix_ref, acc_ref, out_ref):
    full = jnp.concatenate([slab_ref[...], halo_ref[...]], axis=1)
    rows = slab_ref.shape[0]
    blocks = SPAN // LANE
    bases = band_ref.shape[1] // LANE
    windows = jnp.concatenate(
        [full[:, block * LANE : block * LANE + 2 * LANE] for block in range(blocks)], axis=0
    )
    filtered = jnp.dot(windows, band_ref[...], preferred_element_type=jnp.float32)
    filtered = filtered.astype(jnp.bfloat16)
    stacked = jnp.concatenate(
        [
            jnp.concatenate(
                [
                    filtered[block * rows : (block + 1) * rows, base * LANE : (base + 1) * LANE]
                    for block in range(blocks)
                ],
                axis=1,
            )
            for base in range(bases)
        ],
        axis=0,
    )
    out_ref[...] = acc_ref[...] + jnp.dot(mix_ref[...], stacked, preferred_element_type=jnp.float32)


def filter_mix(slab_image, tap_values, mix_matrix, acc):
    rows, width = slab_image.shape
    bases, taps = tap_values.shape
    padded = jnp.pad(slab_image, ((0, 0), (32, SPAN - 32)))
    band_rows = jnp.pad(tap_values, ((0, 0), (15, 2 * LANE + 1 - 15 - taps)))
    band = toeplitz(band_rows, LANE).transpose(2, 0, 1).reshape(2 * LANE, bases * LANE)
    steps = width // SPAN
    return pl.pallas_call(
        filter_mix_kernel,
        grid=(steps,),
        in_specs=[
            pl.BlockSpec((rows, SPAN), lambda k: (0, k)),
            pl.BlockSpec((rows, LANE), lambda k: (0, (k + 1) * (SPAN // LANE))),
            pl.BlockSpec((2 * LANE, bases * LANE), lambda k: (0, 0)),
            pl.BlockSpec((rows, bases * rows), lambda k: (0, 0)),
            pl.BlockSpec((rows, SPAN), lambda k: (0, k)),
        ],
        out_specs=pl.BlockSpec((rows, SPAN), lambda k: (0, k)),
        out_shape=jax.ShapeDtypeStruct((rows, width), jnp.float32),
        input_output_aliases={4: 0},
        cost_estimate=pl.CostEstimate(
            flops=2 * rows * width * 2 * LANE * bases + 2 * rows * width * bases * rows,
            transcendentals=0,
            bytes_accessed=padded.size * 2 + band.size * 2 + mix_matrix.size * 2 + acc.size * 8,
        ),
    )(padded, padded, band, mix_matrix, acc)


def visit_term(received, recv_off, shifts, weight, psf_index, coef_table, basis_x, basis_y, acc):
    warp_x = lanczos_taps(shifts[0])
    warp_y = lanczos_taps(shifts[1])
    slab_image = place(received, recv_off, warp_y).astype(jnp.bfloat16)
    tap_values = combined_taps(basis_x, warp_x).astype(jnp.bfloat16)
    class_hits = (psf_index == jnp.arange(coef_table.shape[0], dtype=jnp.int32)).astype(jnp.float32)
    coeffs = jnp.sum(class_hits[:, None] * coef_table, axis=0)
    mix_matrix = mixing(weight, coeffs, basis_y, SLAB_ROWS)
    return filter_mix(slab_image, tap_values, mix_matrix, acc)


def across_pairs(halves, rows):
    return [(h * rows + r, (halves - 1 - h) * rows + r) for h in range(halves) for r in range(rows)]


def shards(
    exposures, owners, offsets, visit_shift, visit_weight, psf_class, coef_table, basis_x, basis_y
):
    places = lax.axis_size(("x", "y"))
    halves = lax.axis_size("zh")
    rows_z = lax.axis_size("zl")
    streams = rows_z * lax.axis_size("c")
    half = lax.axis_index("zh")
    step_count = exposures.shape[0]
    width = exposures.shape[4]
    strip_rows = exposures.shape[3]
    fanout = owners.shape[3]
    strip_count = exposures.shape[2]
    table = jnp.concatenate([owners[:, 0], offsets[:, 0]], axis=2).reshape(-1)
    table_strip = jnp.zeros((1, strip_rows, width), exposures.dtype)
    table_strip = table_strip.at[0, 0, : table.shape[0]].set(table.astype(exposures.dtype))
    far_strips = []
    for step_index in range(step_count):
        strips = exposures[step_index, 0]
        if step_index == 0:
            strips = jnp.concatenate([strips, table_strip], axis=0)
        elif step_index > 1:
            strips, _ = lax.optimization_barrier((strips, far_strips[step_index - 2]))
        far_strips.append(lax.ppermute(strips, ("zh", "zl"), across_pairs(halves, rows_z)))
    far_table = far_strips[0][strip_count, 0, : table.shape[0]].astype(jnp.int32)
    far_table = far_table.reshape(step_count, strip_count, 2 * fanout)
    own = [
        pack(exposures[step_index, 0], owners[step_index, 0], offsets[step_index, 0], half, places)
        for step_index in range(step_count)
    ]
    far = [
        pack(
            far_strips[step_index][:strip_count],
            far_table[step_index, :, :fanout],
            far_table[step_index, :, fanout:],
            half,
            places,
        )
        for step_index in range(step_count)
    ]
    slot_offsets = jnp.stack(
        [jnp.concatenate([own[t][1], far[t][1]], axis=1) for t in range(step_count)], axis=1
    )
    outgoing = [
        jnp.concatenate([own[step_index][0], far[step_index][0]], axis=1)
        for step_index in range(step_count)
    ]
    received = [None] * step_count
    for step_index in range(min(2, step_count)):
        released = outgoing[step_index]
        if 0 < step_index < step_count - 1:
            released, _ = lax.optimization_barrier((released, far_strips[step_index + 1]))
        received[step_index] = lax.all_to_all(
            released, ("x", "y"), split_axis=0, concat_axis=0, tiled=True
        )
    slot_offsets, _ = lax.optimization_barrier((slot_offsets, received[0]))
    recv_offsets = lax.all_to_all(slot_offsets, ("x", "y"), split_axis=0, concat_axis=0, tiled=True)
    partial_sum = jnp.zeros((SLAB_ROWS, width), jnp.float32)
    for step_index in range(step_count):
        partial_sum = visit_term(
            received[step_index],
            recv_offsets[:, step_index],
            visit_shift[step_index, 0],
            visit_weight[step_index, 0],
            psf_class[step_index, 0],
            coef_table,
            basis_x,
            basis_y,
            partial_sum,
        )
        later = step_index + 2
        if later < step_count:
            released, partial_sum = lax.optimization_barrier((outgoing[later], partial_sum))
            if later < step_count - 1:
                released, _ = lax.optimization_barrier((released, far_strips[later + 1]))
            received[later] = lax.all_to_all(
                released, ("x", "y"), split_axis=0, concat_axis=0, tiled=True
            )
    share_rows = SLAB_ROWS // streams
    pieces = lax.all_to_all(
        partial_sum.astype(jnp.bfloat16).reshape(streams, share_rows, width), ("zl", "c"),
        split_axis=0, concat_axis=0, tiled=True,
    )
    return jnp.sum(pieces.astype(jnp.float32), axis=0)


def solution(mesh):
    names = ("x", "y", "zh", "zl", "c")
    patches, streams = mesh.devices.shape
    fine = Mesh(mesh.devices.reshape(4, 4, patches // 16, streams // 2, 2), names)
    patch = ("x", "y", "zh")
    stream = ("zl", "c")
    placed = (
        P(None, stream, patch, None, None),
        P(None, stream, patch, None),
        P(None, stream, patch, None),
        P(None, stream, None),
        P(None, stream),
        P(None, stream),
        P(),
        P(),
        P(),
    )
    return jax.shard_map(
        shards, mesh=fine, in_specs=placed, out_specs=P(patch + stream, None), check_vma=False
    )
```
